256 devices in a mesh: ctx: 16 (over y_lo, x, core), ch: 16 (over z, y_hi).
Axes of the slice: x: 4, y: 4 (y_hi: 2, y_lo: 2; y = y_hi * 2 + y_lo), z: 8, core: 2. Of those that a mesh axis runs over, the one named last changes fastest.
Arguments:
- tokens: bfloat16 [6144, 4096], P('ctx', 'ch'), may hold values from -2.5 to 2.5
- mr_gain: float32 [4096], replicated, may hold values from 0.1 to 1.9
- mr_inproj: bfloat16 [4096, 3, 4096], P('ctx', None, 'ch'), may hold values from -0.09375 to 0.09375
- mr_outproj: bfloat16 [4096, 4096], P('ch', 'ctx'), may hold values from -0.09375 to 0.09375
- mr_filter: float32 [128, 4096], P(None, 'ch'), may hold values from -0.5 to 0.5
- li_gain: float32 [4096], replicated, may hold values from 0.1 to 1.9
- li_inproj: bfloat16 [4096, 3, 4096], P('ctx', None, 'ch'), may hold values from -0.09375 to 0.09375
- li_outproj: bfloat16 [4096, 4096], P('ch', 'ctx'), may hold values from -0.09375 to 0.09375
- li_decay: float32 [16, 4096], P(None, 'ch'), may hold values from 8.138021e-07 to 0.125
- li_residue: float32 [16, 4096], P(None, 'ch'), may hold values from -1 to 1
- doc_ids: int32 [6144], replicated, may hold values from 0 to 3, never falling along the last dimension, each value on 1 to 3072 neighbouring positions
Outputs:
- layer_out: bfloat16 [6144, 4096], P('ctx', 'ch')
The draws below stay inside these ranges and needn't reach their ends.
Inputs may be any that keep to these rules, and one draw needn't show every extreme that they name: `doc_ids`: ids never fall along the sequence and every one of the 4 ids occurs.
All inputs are finite; a program needn't handle non-finite values.
Results may differ from the reference program's by a relative error of at most 0.03.
Values may be sent and summed in bfloat16 or wider, within the bound.
No kernel may reach another device: no remote copies, remote signals or barrier semaphores. Data moves between devices by JAX's collectives and lax.ppermute only.
A program may use at most 128 MiB of HBM per device.

```python
import math
import jax
import jax.numpy as jnp
import numpy as np
from jax import lax

D = 4096
MODES = 16
MR_TAPS = 128
DOCS = 4
TOKENS = 6144
N_CTX = 16
N_CH = 16


def log_between(uniform_draw, lowest, highest):
    return jnp.exp(math.log(lowest) + uniform_draw * (math.log(highest) - math.log(lowest)))


def decay_rates(key):
    uniform_draw = jax.random.uniform(jax.random.fold_in(key, 101), (MODES, D), jnp.float32)
    return log_between(uniform_draw, min(2.0 / TOKENS, 1.0 / 64.0), 1.0 / 32.0)


def draw_li_decay(key, part):
    return decay_rates(key)


def draw_li_residue(key, part):
    rates = decay_rates(key)
    base_draw = jnp.clip(jax.random.normal(jax.random.fold_in(key, 202), (MODES, D), jnp.float32), -2.5, 2.5)
    scale = jnp.sqrt(jnp.maximum(2.0 * rates, 8.0 / TOKENS) / MODES) * 1.5
    return jnp.clip(base_draw * scale, -1.0, 1.0)


def level_of(own_key, extent, shards, low, high):
    loudness, own = 1.0, jax.random.fold_in(own_key, 6)
    for axis_at, blocks in shards:
        heights = jnp.exp(jax.random.uniform(jax.random.fold_in(own, axis_at), (blocks,), jnp.float32, low / len(shards), high / len(shards)))
        loudness = loudness * jnp.repeat(heights, extent[axis_at] // blocks).reshape([-1 if axis == axis_at else 1 for axis in range(len(extent))])
    return loudness


def length_profile(number_of, total, limit, skew):
    loads = [(1 << 20) // math.isqrt(standing ** skew) + 1 for standing in range(2, number_of + 1)]
    rest, given = total - limit - (number_of - 1), [1] * (number_of - 1)
    while rest > 0:
        candidates = [i for i in range(number_of - 1) if given[i] < limit]
        mass, left = sum([loads[i] for i in candidates]), rest
        for i in candidates:
            more = min(limit - given[i], max(1, left * loads[i] // mass), rest)
            given[i] = given[i] + more
            rest = rest - more
    return np.array([limit] + given)


def uneven_parts(rng, amount, total, reach, lean):
    if amount == 2:
        one = jax.random.randint(rng, (), max(1, total - reach), min(reach, total - 1) + 1)
        return jnp.stack([one, total - one])
    sizes = jnp.asarray(length_profile(amount, total, reach, lean), jnp.int32)
    twos = (amount - 1) // 2
    giver, receiver = sizes[1:1 + 2 * twos:2], sizes[2:2 + 2 * twos:2]
    room = jnp.minimum(giver - 1, reach - receiver)
    passed = jax.random.randint(jax.random.fold_in(rng, 1), (twos,), 0, 1 << 20) % (room + 1)
    sizes = sizes.at[1:1 + 2 * twos:2].set(giver - passed).at[2:2 + 2 * twos:2].set(receiver + passed)
    return sizes[jax.random.permutation(jax.random.fold_in(rng, 2), amount)]


def gaussian(stream_key, shape, scale, reach, shards=(), kind=jnp.bfloat16):
    values = scale * jax.random.normal(stream_key, shape, jnp.float32)
    if shards:
        values = values * level_of(stream_key, shape, shards, -0.22, 0.18)
    return jnp.clip(values, -reach, reach).astype(kind)


def setup_inputs(seed: int = 0) -> dict:
    splits = jax.random.split(jax.random.key(seed), 12)
    tokens = gaussian(splits[0], (TOKENS, D), 0.25, 2.5, ((0, 16), (1, 16)))
    mr_gain = jnp.clip(1.0 + 0.18 * jax.random.normal(splits[1], (D,), jnp.float32), 0.1, 1.9)
    mr_inproj = gaussian(splits[2], (D, 3, D), D ** -0.5, 0.09375, ((0, 16), (2, 16)))
    mr_outproj = gaussian(splits[3], (D, D), D ** -0.5, 0.09375, ((0, 16), (1, 16)))
    mr_filter = gaussian(splits[4], (MR_TAPS, D), MR_TAPS ** -0.5, 0.5, ((1, 16),), jnp.float32)
    li_gain = jnp.clip(1.0 + 0.18 * jax.random.normal(splits[5], (D,), jnp.float32), 0.1, 1.9)
    li_inproj = gaussian(splits[6], (D, 3, D), D ** -0.5, 0.09375, ((0, 16), (2, 16)))
    li_outproj = gaussian(splits[7], (D, D), D ** -0.5, 0.09375, ((0, 16), (1, 16)))
    li_decay = draw_li_decay(jax.random.fold_in(splits[11], 71), 0)
    li_residue = draw_li_residue(jax.random.fold_in(splits[11], 71), 0)
    doc_ids = jnp.searchsorted(jnp.cumsum(uneven_parts(splits[10], DOCS, TOKENS, TOKENS // 2, 2)), jnp.arange(TOKENS), side="right").astype(jnp.int32)
    return {"tokens": tokens, "mr_gain": mr_gain, "mr_inproj": mr_inproj, "mr_outproj": mr_outproj, "mr_filter": mr_filter, "li_gain": li_gain, "li_inproj": li_inproj, "li_outproj": li_outproj, "li_decay": li_decay, "li_residue": li_residue, "doc_ids": doc_ids}


def to_sequence(stored):
    blocks = stored.reshape((N_CTX, 2, stored.shape[0] // (2 * N_CTX)) + stored.shape[1:])
    return jnp.concatenate([blocks[:, 0], blocks[::-1, 1]], 0).reshape(stored.shape)

def to_stored(ordered):
    blocks = ordered.reshape((2 * N_CTX, ordered.shape[0] // (2 * N_CTX)) + ordered.shape[1:])
    return jnp.stack([blocks[:N_CTX], blocks[N_CTX:][::-1]], 1).reshape(ordered.shape)

def project_in(stream, gain, inproj):
    floats = stream.astype(jnp.float32)
    scaled = lax.rsqrt(lax.optimization_barrier(jnp.mean(floats * floats, axis=1, keepdims=True)) + 1e-06)
    normed = (floats * scaled * gain[None, :]).astype(jnp.bfloat16)
    joined = jnp.dot(normed, inproj.reshape(D, 3 * D), preferred_element_type=jnp.float32).astype(jnp.bfloat16)
    product = (joined[:, D:2 * D].astype(jnp.float32) * joined[:, 2 * D:].astype(jnp.float32)).astype(jnp.bfloat16)
    return (joined[:, :D], product)

def project_out(stream, query, mixed, outproj):
    gated = (query.astype(jnp.float32) * mixed).astype(jnp.bfloat16)
    group = D // N_CH

    def add_group(number, running):
        begin = (number * group).astype(jnp.int32)
        columns = lax.dynamic_slice_in_dim(gated, begin, group, 1)
        weights = lax.dynamic_slice_in_dim(outproj, begin, group, 0)
        partial_sum = jnp.dot(columns, weights, preferred_element_type=jnp.float32).astype(jnp.bfloat16)
        partial_sum = lax.optimization_barrier(partial_sum)
        return running + partial_sum.astype(jnp.float32)
    summed = lax.fori_loop(0, N_CH, add_group, jnp.zeros((TOKENS, D), jnp.float32))
    return (stream.astype(jnp.float32) + summed).astype(jnp.bfloat16)

def short_mix(product, mr_filter, doc_ids):
    floats = product.astype(jnp.float32)
    places = jnp.arange(TOKENS)

    def add_tap(tap_lag, running):
        moved = jnp.roll(floats, tap_lag, axis=0)
        moved_docs = jnp.roll(doc_ids, tap_lag)
        keep = (places >= tap_lag) & (moved_docs == doc_ids)
        weight = lax.dynamic_slice_in_dim(mr_filter, jnp.asarray(tap_lag).astype(jnp.int32), 1, 0)
        return running + jnp.where(keep[:, None], moved, 0.0) * weight
    return lax.fori_loop(0, MR_TAPS, add_tap, jnp.zeros((TOKENS, D), jnp.float32))

def combine_pairs(early, late):
    return (early[0] * late[0], late[0] * early[1] + late[1])

def long_mix(product, li_decay, li_residue, doc_ids):
    group = D // N_CH
    follows = jnp.concatenate([jnp.zeros((1,), bool), doc_ids[1:] == doc_ids[:-1]])

    def one_group(number):
        begin = (number * group).astype(jnp.int32)
        columns = lax.dynamic_slice_in_dim(product, begin, group, 1).astype(jnp.float32)
        rates = lax.dynamic_slice_in_dim(li_decay, begin, group, 1)
        weights = lax.dynamic_slice_in_dim(li_residue, begin, group, 1)
        carried = jnp.where(follows[:, None, None], jnp.exp(-rates)[None], 0.0)
        inputs = jnp.broadcast_to(columns[:, None, :], carried.shape)
        _, states = lax.associative_scan(combine_pairs, (carried, inputs), axis=0)
        return jnp.einsum('tmc,mc->tc', states, weights)
    parts = lax.map(one_group, jnp.arange(N_CH, dtype=jnp.int32))
    return jnp.transpose(parts, (1, 0, 2)).reshape(TOKENS, D)

def reference(tokens, mr_gain, mr_inproj, mr_outproj, mr_filter, li_gain, li_inproj, li_outproj, li_decay, li_residue, doc_ids):
    stream = to_sequence(tokens)
    query, product = project_in(stream, mr_gain, mr_inproj)
    stream = project_out(stream, query, short_mix(product, mr_filter, doc_ids), mr_outproj)
    query, product = project_in(stream, li_gain, li_inproj)
    stream = project_out(stream, query, long_mix(product, li_decay, li_residue, doc_ids), li_outproj)
    return to_stored(stream)
```

```python
import math

import jax
import jax.numpy as jnp
from jax import lax
from jax.experimental import pallas as pl
from jax.experimental.pallas import tpu as pltpu
from jax.sharding import PartitionSpec as P


def extended(value, sides, width):
    for axis, dim in sides:
        count, length = (lax.axis_size(axis), value.shape[dim])
        up = [(i, (i + 1) % count) for i in range(count - 1)]
        down = [(j, i) for i, j in up]
        last = lax.slice_in_dim(value, length - width, length, axis=dim)
        initial = lax.slice_in_dim(value, 0, width, axis=dim)
        before = lax.ppermute(last, axis, up)
        after = lax.ppermute(initial, axis, down)
        value = jnp.concatenate([before, value, after], axis=dim)
    return value


def features_in(stream, gain, inproj):
    whole = lax.all_gather(stream, "ch", axis=1, tiled=True)
    floats = whole.astype(jnp.float32)
    scaled = lax.rsqrt(jnp.mean(floats * floats, axis=1, keepdims=True) + 1e-06)
    normed = (floats * scaled * gain[None, :]).astype(jnp.bfloat16)
    channels = inproj.shape[2]
    piece = lax.all_gather(inproj, "ctx", axis=0, tiled=True)
    flat = piece.reshape(piece.shape[0], 3 * channels)
    joined = jnp.dot(normed, flat, preferred_element_type=jnp.float32).astype(jnp.bfloat16)
    product = (
        joined[:, channels : 2 * channels].astype(jnp.float32)
        * joined[:, 2 * channels :].astype(jnp.float32)
    ).astype(jnp.bfloat16)
    return (joined[:, :channels], product)


def outproj_columns(outproj):
    ctx_count, ch_count = (lax.axis_size("ctx"), lax.axis_size("ch"))
    assert ctx_count == ch_count
    pairs = [(i * ch_count + c, c * ch_count + i) for i in range(ctx_count) for c in range(ch_count)]
    swapped = lax.ppermute(outproj, ("ctx", "ch"), pairs)
    return lax.all_gather(swapped, "ctx", axis=0, tiled=True)


def features_out(stream, query, mixed, columns):
    gated = (query.astype(jnp.float32) * mixed).astype(jnp.bfloat16)
    whole = lax.all_gather(gated, "ch", axis=1, tiled=True)
    rows, width = gated.shape
    groups = whole.shape[1] // width
    parts = jnp.einsum(
        "tgk,gkj->gtj",
        whole.reshape(rows, groups, width),
        columns.reshape(groups, width, columns.shape[1]),
        preferred_element_type=jnp.float32,
    ).astype(jnp.bfloat16)
    summed = jnp.sum(parts.astype(jnp.float32), axis=0)
    return (stream.astype(jnp.float32) + summed).astype(jnp.bfloat16)


def span_layout(shard_rows):
    ctx_count = lax.axis_size("ctx")
    ctx_index = lax.axis_index("ctx")
    span_rows = shard_rows // 2
    span_starts = jnp.stack([ctx_index * span_rows, (2 * ctx_count - 1 - ctx_index) * span_rows])
    positions = span_starts[:, None] + jnp.arange(span_rows)[None, :]
    return (ctx_count, ctx_index, span_rows, span_starts, positions)


def short_mix(product, mr_filter, doc_ids):
    shard_rows, channels = product.shape
    ctx_count, ctx_index, span_rows, span_starts, positions = span_layout(shard_rows)
    tap_count = mr_filter.shape[0]
    reach_rows = tap_count - 1
    halves = product.reshape(2, span_rows, channels)
    tails = jnp.concatenate(
        [halves[1, span_rows - reach_rows :], halves[0, span_rows - reach_rows :]], 0
    )
    framed = extended(tails, (("ctx", 0),), reach_rows)
    before_upper = jnp.where(
        ctx_index == ctx_count - 1, halves[0, span_rows - reach_rows :], framed[3 * reach_rows :]
    )
    lower_window = jnp.concatenate([framed[:reach_rows], halves[0]], 0)
    upper_window = jnp.concatenate([before_upper, halves[1]], 0)
    windows = jnp.stack([lower_window, upper_window]).astype(jnp.float32)
    window_places = span_starts[:, None] - reach_rows + jnp.arange(reach_rows + span_rows)[None, :]
    window_docs = jnp.where(
        window_places >= 0, jnp.take(doc_ids, jnp.clip(window_places, 0, None)), -1
    )
    target_docs = window_docs[:, reach_rows:]
    tap_block = math.gcd(tap_count, 16)

    def tap_group(group_number, running):
        for offset in range(tap_block):
            tap_lag = group_number * tap_block + offset
            source = lax.dynamic_slice_in_dim(windows, reach_rows - tap_lag, span_rows, 1)
            source_docs = lax.dynamic_slice_in_dim(window_docs, reach_rows - tap_lag, span_rows, 1)
            weight = lax.dynamic_slice_in_dim(mr_filter, tap_lag, 1, 0)
            running = (
                running
                + jnp.where((source_docs == target_docs)[:, :, None], source, 0.0) * weight[None]
            )
        return running

    mixed = lax.fori_loop(
        0, tap_count // tap_block, tap_group, jnp.zeros((2, span_rows, channels), jnp.float32)
    )
    return mixed.reshape(shard_rows, channels)


def scan_kernel(flags_ref, x_ref, factor_ref, init_ref, residue_ref, mixed_ref, end_ref):
    halves, span_rows, _ = x_ref.shape
    factor = factor_ref[...]
    residue = residue_ref[...]
    for half in range(halves):

        def step(t, state):
            kept = factor * flags_ref[half * span_rows + t]
            state = kept * state + x_ref[half, pl.ds(t, 1), :]
            mixed_ref[half, pl.ds(t, 1), :] = jnp.sum(residue * state, axis=0, keepdims=True)
            return state

        end_ref[half] = lax.fori_loop(0, span_rows, step, init_ref[half], unroll=8)


def run_scan(flags, values, factor, init, residue):
    halves, span_rows, channels = values.shape
    modes = factor.shape[0]
    vmem = pl.BlockSpec(memory_space=pltpu.VMEM)
    steps = halves * span_rows * modes * channels
    return pl.pallas_call(
        scan_kernel,
        out_shape=(
            jax.ShapeDtypeStruct((halves, span_rows, channels), jnp.float32),
            jax.ShapeDtypeStruct((halves, modes, channels), jnp.float32),
        ),
        in_specs=[pl.BlockSpec(memory_space=pltpu.SMEM), vmem, vmem, vmem, vmem],
        out_specs=(vmem, vmem),
        cost_estimate=pl.CostEstimate(
            flops=5 * steps, transcendentals=0, bytes_accessed=8 * halves * span_rows * channels
        ),
    )(flags, values, factor, init, residue)


def long_mix(product, li_decay, li_residue, doc_ids):
    shard_rows, channels = product.shape
    ctx_count, ctx_index, span_rows, span_starts, positions = span_layout(shard_rows)
    modes = li_decay.shape[0]
    own_docs = jnp.take(doc_ids, positions)
    prior_docs = jnp.take(doc_ids, jnp.clip(positions - 1, 0, None))
    flags = ((positions > 0) & (own_docs == prior_docs)).astype(jnp.float32).reshape(-1)
    factor = jnp.exp(-li_decay)
    values = product.reshape(2, span_rows, channels).astype(jnp.float32)
    zeros = jnp.zeros((2, modes, channels), jnp.float32)
    _, ends = run_scan(flags, values, factor, zeros, li_residue)
    gathered = lax.all_gather(ends, "ctx", axis=0, tiled=False)
    block_ends = jnp.concatenate([gathered[:, 0], gathered[::-1, 1]], 0)
    block_count = 2 * ctx_count
    blocks = jnp.arange(block_count)
    end_docs = jnp.take(doc_ids, (blocks + 1) * span_rows - 1)
    targets = span_starts // span_rows
    entry_docs = jnp.take(doc_ids, jnp.clip(span_starts - 1, 0, None))
    linked = (blocks[None, :] < targets[:, None]) & (end_docs[None, :] == entry_docs[:, None])
    distance = jnp.where(linked, (targets[:, None] - blocks[None, :] - 1) * span_rows, 0).astype(jnp.float32)
    weights = jnp.exp(-li_decay[None, None] * distance[:, :, None, None]) * linked.astype(jnp.float32)[:, :, None, None]
    entry = jnp.sum(weights * block_ends[None], axis=1)
    mixed, _ = run_scan(flags, values, factor, entry, li_residue)
    return mixed.reshape(shard_rows, channels)


def body(
    tokens,
    mr_gain,
    mr_inproj,
    mr_outproj,
    mr_filter,
    li_gain,
    li_inproj,
    li_outproj,
    li_decay,
    li_residue,
    doc_ids,
):
    mr_columns = outproj_columns(mr_outproj)
    li_columns = outproj_columns(li_outproj)
    query, product = features_in(tokens, mr_gain, mr_inproj)
    stream = features_out(tokens, query, short_mix(product, mr_filter, doc_ids), mr_columns)
    query, product = features_in(stream, li_gain, li_inproj)
    return features_out(stream, query, long_mix(product, li_decay, li_residue, doc_ids), li_columns)


def solution(mesh):
    in_specs = (
        P("ctx", "ch"),
        P(),
        P("ctx", None, "ch"),
        P("ch", "ctx"),
        P(None, "ch"),
        P(),
        P("ctx", None, "ch"),
        P("ch", "ctx"),
        P(None, "ch"),
        P(None, "ch"),
        P(),
    )
    out_specs = P("ctx", "ch")
    return jax.shard_map(body, mesh=mesh, in_specs=in_specs, out_specs=out_specs, check_vma=False)
```

```python
import math

import jax
import jax.numpy as jnp
from jax import lax
from jax.experimental import pallas as pl
from jax.experimental.pallas import tpu as pltpu
from jax.sharding import PartitionSpec as P


def extended(value, sides, width):
    for axis, dim in sides:
        count, length = (lax.axis_size(axis), value.shape[dim])
        up = [(i, (i + 1) % count) for i in range(count - 1)]
        down = [(j, i) for i, j in up]
        last = lax.slice_in_dim(value, length - width, length, axis=dim)
        initial = lax.slice_in_dim(value, 0, width, axis=dim)
        before = lax.ppermute(last, axis, up)
        after = lax.ppermute(initial, axis, down)
        value = jnp.concatenate([before, value, after], axis=dim)
    return value


CH = ("z", "yh")


def gather_channels(value):
    pair = lax.all_gather(value, "yh", axis=1, tiled=True)
    return lax.all_gather(pair, "z", axis=1, tiled=True)


def features_in(stream, gain, inproj):
    whole = gather_channels(stream)
    floats = whole.astype(jnp.float32)
    scaled = lax.rsqrt(jnp.mean(floats * floats, axis=1, keepdims=True) + 1e-06)
    normed = (floats * scaled * gain[None, :]).astype(jnp.bfloat16)
    channels = inproj.shape[2]
    piece = lax.all_gather(inproj, "ctx", axis=0, tiled=True)
    flat = piece.reshape(piece.shape[0], 3 * channels)
    joined = jnp.dot(normed, flat, preferred_element_type=jnp.float32).astype(jnp.bfloat16)
    product = (
        joined[:, channels : 2 * channels].astype(jnp.float32)
        * joined[:, 2 * channels :].astype(jnp.float32)
    ).astype(jnp.bfloat16)
    return (joined[:, :channels], product)


def outproj_columns(outproj):
    ctx_count, ch_count = (lax.axis_size("ctx"), lax.axis_size(CH))
    assert ctx_count == ch_count
    pairs = [(i * ch_count + c, c * ch_count + i) for i in range(ctx_count) for c in range(ch_count)]
    swapped = lax.ppermute(outproj, ("ctx",) + CH, pairs)
    return lax.all_gather(swapped, "ctx", axis=0, tiled=True)


def features_out(stream, query, mixed, columns):
    gated = (query.astype(jnp.float32) * mixed).astype(jnp.bfloat16)
    whole = gather_channels(gated)
    rows, width = gated.shape
    groups = whole.shape[1] // width
    parts = jnp.einsum(
        "tgk,gkj->gtj",
        whole.reshape(rows, groups, width),
        columns.reshape(groups, width, columns.shape[1]),
        preferred_element_type=jnp.float32,
    ).astype(jnp.bfloat16)
    summed = jnp.sum(parts.astype(jnp.float32), axis=0)
    return (stream.astype(jnp.float32) + summed).astype(jnp.bfloat16)


def span_layout(shard_rows):
    ctx_count = lax.axis_size("ctx")
    ctx_index = lax.axis_index("ctx")
    span_rows = shard_rows // 2
    span_starts = jnp.stack([ctx_index * span_rows, (2 * ctx_count - 1 - ctx_index) * span_rows])
    positions = span_starts[:, None] + jnp.arange(span_rows)[None, :]
    return (ctx_count, ctx_index, span_rows, span_starts, positions)


def short_mix(product, mr_filter, doc_ids):
    shard_rows, channels = product.shape
    ctx_count, ctx_index, span_rows, span_starts, positions = span_layout(shard_rows)
    tap_count = mr_filter.shape[0]
    reach_rows = tap_count - 1
    halves = product.reshape(2, span_rows, channels)
    tails = jnp.concatenate(
        [halves[1, span_rows - reach_rows :], halves[0, span_rows - reach_rows :]], 0
    )
    framed = extended(tails, (("ctx", 0),), reach_rows)
    before_upper = jnp.where(
        ctx_index == ctx_count - 1, halves[0, span_rows - reach_rows :], framed[3 * reach_rows :]
    )
    lower_window = jnp.concatenate([framed[:reach_rows], halves[0]], 0)
    upper_window = jnp.concatenate([before_upper, halves[1]], 0)
    windows = jnp.stack([lower_window, upper_window]).astype(jnp.float32)
    window_places = span_starts[:, None] - reach_rows + jnp.arange(reach_rows + span_rows)[None, :]
    window_docs = jnp.where(
        window_places >= 0, jnp.take(doc_ids, jnp.clip(window_places, 0, None)), -1
    )
    target_docs = window_docs[:, reach_rows:]
    tap_block = math.gcd(tap_count, 16)

    def tap_group(group_number, running):
        for offset in range(tap_block):
            tap_lag = group_number * tap_block + offset
            source = lax.dynamic_slice_in_dim(windows, reach_rows - tap_lag, span_rows, 1)
            source_docs = lax.dynamic_slice_in_dim(window_docs, reach_rows - tap_lag, span_rows, 1)
            weight = lax.dynamic_slice_in_dim(mr_filter, tap_lag, 1, 0)
            running = (
                running
                + jnp.where((source_docs == target_docs)[:, :, None], source, 0.0) * weight[None]
            )
        return running

    mixed = lax.fori_loop(
        0, tap_count // tap_block, tap_group, jnp.zeros((2, span_rows, channels), jnp.float32)
    )
    return mixed.reshape(shard_rows, channels)


def scan_kernel(flags_ref, x_ref, factor_ref, init_ref, residue_ref, mixed_ref, end_ref):
    halves, span_rows, _ = x_ref.shape
    factor = factor_ref[...]
    residue = residue_ref[...]
    for half in range(halves):

        def step(t, state):
            kept = factor * flags_ref[half * span_rows + t]
            state = kept * state + x_ref[half, pl.ds(t, 1), :]
            mixed_ref[half, pl.ds(t, 1), :] = jnp.sum(residue * state, axis=0, keepdims=True)
            return state

        end_ref[half] = lax.fori_loop(0, span_rows, step, init_ref[half], unroll=8)


def run_scan(flags, values, factor, init, residue):
    halves, span_rows, channels = values.shape
    modes = factor.shape[0]
    vmem = pl.BlockSpec(memory_space=pltpu.VMEM)
    steps = halves * span_rows * modes * channels
    return pl.pallas_call(
        scan_kernel,
        out_shape=(
            jax.ShapeDtypeStruct((halves, span_rows, channels), jnp.float32),
            jax.ShapeDtypeStruct((halves, modes, channels), jnp.float32),
        ),
        in_specs=[pl.BlockSpec(memory_space=pltpu.SMEM), vmem, vmem, vmem, vmem],
        out_specs=(vmem, vmem),
        cost_estimate=pl.CostEstimate(
            flops=5 * steps, transcendentals=0, bytes_accessed=8 * halves * span_rows * channels
        ),
    )(flags, values, factor, init, residue)


def long_mix(product, li_decay, li_residue, doc_ids):
    shard_rows, channels = product.shape
    ctx_count, ctx_index, span_rows, span_starts, positions = span_layout(shard_rows)
    modes = li_decay.shape[0]
    own_docs = jnp.take(doc_ids, positions)
    prior_docs = jnp.take(doc_ids, jnp.clip(positions - 1, 0, None))
    flags = ((positions > 0) & (own_docs == prior_docs)).astype(jnp.float32).reshape(-1)
    factor = jnp.exp(-li_decay)
    values = product.reshape(2, span_rows, channels).astype(jnp.float32)
    zeros = jnp.zeros((2, modes, channels), jnp.float32)
    _, ends = run_scan(flags, values, factor, zeros, li_residue)
    gathered = lax.all_gather(ends, "ctx", axis=0, tiled=False)
    block_ends = jnp.concatenate([gathered[:, 0], gathered[::-1, 1]], 0)
    block_count = 2 * ctx_count
    blocks = jnp.arange(block_count)
    end_docs = jnp.take(doc_ids, (blocks + 1) * span_rows - 1)
    targets = span_starts // span_rows
    entry_docs = jnp.take(doc_ids, jnp.clip(span_starts - 1, 0, None))
    linked = (blocks[None, :] < targets[:, None]) & (end_docs[None, :] == entry_docs[:, None])
    distance = jnp.where(linked, (targets[:, None] - blocks[None, :] - 1) * span_rows, 0).astype(jnp.float32)
    weights = jnp.exp(-li_decay[None, None] * distance[:, :, None, None]) * linked.astype(jnp.float32)[:, :, None, None]
    entry = jnp.sum(weights * block_ends[None], axis=1)
    mixed, _ = run_scan(flags, values, factor, entry, li_residue)
    return mixed.reshape(shard_rows, channels)


def body(
    tokens,
    mr_gain,
    mr_inproj,
    mr_outproj,
    mr_filter,
    li_gain,
    li_inproj,
    li_outproj,
    li_decay,
    li_residue,
    doc_ids,
):
    mr_columns = outproj_columns(mr_outproj)
    li_columns = outproj_columns(li_outproj)
    query, product = features_in(tokens, mr_gain, mr_inproj)
    stream = features_out(tokens, query, short_mix(product, mr_filter, doc_ids), mr_columns)
    query, product = features_in(stream, li_gain, li_inproj)
    return features_out(stream, query, long_mix(product, li_decay, li_residue, doc_ids), li_columns)


def solution(mesh):
    ctx_count, ch_count = mesh.devices.shape
    pair_count = 2 if ch_count % 2 == 0 else 1
    view = jax.sharding.Mesh(
        mesh.devices.reshape(ctx_count, ch_count // pair_count, pair_count), ("ctx",) + CH
    )
    in_specs = (
        P("ctx", CH),
        P(),
        P("ctx", None, CH),
        P(CH, "ctx"),
        P(None, CH),
        P(),
        P("ctx", None, CH),
        P(CH, "ctx"),
        P(None, CH),
        P(None, CH),
        P(),
    )
    out_specs = P("ctx", CH)
    return jax.shard_map(body, mesh=view, in_specs=in_specs, out_specs=out_specs, check_vma=False)
```

```python
import math

import jax
import jax.numpy as jnp
from jax import lax
from jax.experimental import pallas as pl
from jax.experimental.pallas import tpu as pltpu
from jax.sharding import PartitionSpec as P


def extended(value, sides, width):
    for axis, dim in sides:
        count, length = (lax.axis_size(axis), value.shape[dim])
        up = [(i, (i + 1) % count) for i in range(count - 1)]
        down = [(j, i) for i, j in up]
        last = lax.slice_in_dim(value, length - width, length, axis=dim)
        initial = lax.slice_in_dim(value, 0, width, axis=dim)
        before = lax.ppermute(last, axis, up)
        after = lax.ppermute(initial, axis, down)
        value = jnp.concatenate([before, value, after], axis=dim)
    return value


CH = ("z", "yh")


def gather_channels(value):
    pair = lax.all_gather(value, "yh", axis=1, tiled=True)
    return lax.all_gather(pair, "z", axis=1, tiled=True)


def gather_weights(inproj):
    return lax.all_gather(inproj, "ctx", axis=0, tiled=True)


def features_in(stream, gain, piece):
    whole = gather_channels(stream)
    floats = whole.astype(jnp.float32)
    scaled = lax.rsqrt(jnp.mean(floats * floats, axis=1, keepdims=True) + 1e-06)
    normed = (floats * scaled * gain[None, :]).astype(jnp.bfloat16)
    channels = piece.shape[2]
    flat = piece.reshape(piece.shape[0], 3 * channels)
    joined = jnp.dot(normed, flat, preferred_element_type=jnp.float32).astype(jnp.bfloat16)
    product = (
        joined[:, channels : 2 * channels].astype(jnp.float32)
        * joined[:, 2 * channels :].astype(jnp.float32)
    ).astype(jnp.bfloat16)
    return (joined[:, :channels], product)


def outproj_columns(outproj):
    ctx_count, ch_count = (lax.axis_size("ctx"), lax.axis_size(CH))
    assert ctx_count == ch_count
    pairs = [(i * ch_count + c, c * ch_count + i) for i in range(ctx_count) for c in range(ch_count)]
    swapped = lax.ppermute(outproj, ("ctx",) + CH, pairs)
    return lax.all_gather(swapped, "ctx", axis=0, tiled=True)


def features_out(stream, query, mixed, columns):
    gated = (query.astype(jnp.float32) * mixed).astype(jnp.bfloat16)
    whole = gather_channels(gated)
    rows, width = gated.shape
    groups = whole.shape[1] // width
    parts = jnp.einsum(
        "tgk,gkj->gtj",
        whole.reshape(rows, groups, width),
        columns.reshape(groups, width, columns.shape[1]),
        preferred_element_type=jnp.float32,
    ).astype(jnp.bfloat16)
    summed = jnp.sum(parts.astype(jnp.float32), axis=0)
    return (stream.astype(jnp.float32) + summed).astype(jnp.bfloat16)


def span_layout(shard_rows):
    ctx_count = lax.axis_size("ctx")
    ctx_index = lax.axis_index("ctx")
    span_rows = shard_rows // 2
    span_starts = jnp.stack([ctx_index * span_rows, (2 * ctx_count - 1 - ctx_index) * span_rows])
    positions = span_starts[:, None] + jnp.arange(span_rows)[None, :]
    return (ctx_count, ctx_index, span_rows, span_starts, positions)


def short_mix(product, mr_filter, doc_ids):
    shard_rows, channels = product.shape
    ctx_count, ctx_index, span_rows, span_starts, _ = span_layout(shard_rows)
    tap_count = mr_filter.shape[0]
    reach_rows = tap_count - 1
    halves = product.reshape(2, span_rows, channels)
    tails = jnp.concatenate(
        [halves[1, span_rows - reach_rows :], halves[0, span_rows - reach_rows :]], 0
    )
    framed = extended(tails, (("ctx", 0),), reach_rows)
    before_upper = jnp.where(
        ctx_index == ctx_count - 1, halves[0, span_rows - reach_rows :], framed[3 * reach_rows :]
    )
    lower_window = jnp.concatenate([framed[:reach_rows], halves[0]], 0)
    upper_window = jnp.concatenate([before_upper, halves[1]], 0)
    windows = jnp.stack([lower_window, upper_window]).astype(jnp.float32)
    window_places = span_starts[:, None] - reach_rows + jnp.arange(reach_rows + span_rows)[None, :]
    window_docs = jnp.where(
        window_places >= 0, jnp.take(doc_ids, jnp.clip(window_places, 0, None)), -1
    )
    target_docs = window_docs[:, reach_rows:]
    tap_block = math.gcd(tap_count, 16)

    def tap_group(group_number, running):
        for offset in range(tap_block):
            tap_lag = group_number * tap_block + offset
            source = lax.dynamic_slice_in_dim(windows, reach_rows - tap_lag, span_rows, 1)
            source_docs = lax.dynamic_slice_in_dim(window_docs, reach_rows - tap_lag, span_rows, 1)
            weight = lax.dynamic_slice_in_dim(mr_filter, tap_lag, 1, 0)
            running = (
                running
                + jnp.where((source_docs == target_docs)[:, :, None], source, 0.0) * weight[None]
            )
        return running

    mixed = lax.fori_loop(
        0, tap_count // tap_block, tap_group, jnp.zeros((2, span_rows, channels), jnp.float32)
    )
    return mixed.reshape(shard_rows, channels)


def scan_kernel(flags_ref, x_ref, factor_ref, init_ref, residue_ref, mixed_ref, end_ref):
    halves, span_rows, _ = x_ref.shape
    factor = factor_ref[...]
    residue = residue_ref[...]
    for half in range(halves):

        def step(t, state):
            kept = factor * flags_ref[half * span_rows + t]
            state = kept * state + x_ref[half, pl.ds(t, 1), :]
            mixed_ref[half, pl.ds(t, 1), :] = jnp.sum(residue * state, axis=0, keepdims=True)
            return state

        end_ref[half] = lax.fori_loop(0, span_rows, step, init_ref[half], unroll=8)


def run_scan(flags, values, factor, init, residue):
    halves, span_rows, channels = values.shape
    modes = factor.shape[0]
    vmem = pl.BlockSpec(memory_space=pltpu.VMEM)
    steps = halves * span_rows * modes * channels
    return pl.pallas_call(
        scan_kernel,
        out_shape=(
            jax.ShapeDtypeStruct((halves, span_rows, channels), jnp.float32),
            jax.ShapeDtypeStruct((halves, modes, channels), jnp.float32),
        ),
        in_specs=[pl.BlockSpec(memory_space=pltpu.SMEM), vmem, vmem, vmem, vmem],
        out_specs=(vmem, vmem),
        cost_estimate=pl.CostEstimate(
            flops=5 * steps, transcendentals=0, bytes_accessed=8 * halves * span_rows * channels
        ),
    )(flags, values, factor, init, residue)


def long_mix(product, li_decay, li_residue, doc_ids):
    shard_rows, channels = product.shape
    ctx_count, _, span_rows, span_starts, positions = span_layout(shard_rows)
    modes = li_decay.shape[0]
    own_docs = jnp.take(doc_ids, positions)
    prior_docs = jnp.take(doc_ids, jnp.clip(positions - 1, 0, None))
    flags = ((positions > 0) & (own_docs == prior_docs)).astype(jnp.float32).reshape(-1)
    factor = jnp.exp(-li_decay)
    values = product.reshape(2, span_rows, channels).astype(jnp.float32)
    zeros = jnp.zeros((2, modes, channels), jnp.float32)
    _, ends = run_scan(flags, values, factor, zeros, li_residue)
    gathered = lax.all_gather(ends, "ctx", axis=0, tiled=False)
    block_ends = jnp.concatenate([gathered[:, 0], gathered[::-1, 1]], 0)
    block_count = 2 * ctx_count
    blocks = jnp.arange(block_count)
    end_docs = jnp.take(doc_ids, (blocks + 1) * span_rows - 1)
    targets = span_starts // span_rows
    entry_docs = jnp.take(doc_ids, jnp.clip(span_starts - 1, 0, None))
    linked = (blocks[None, :] < targets[:, None]) & (end_docs[None, :] == entry_docs[:, None])
    distance = jnp.where(linked, (targets[:, None] - blocks[None, :] - 1) * span_rows, 0).astype(jnp.float32)
    weights = jnp.exp(-li_decay[None, None] * distance[:, :, None, None]) * linked.astype(jnp.float32)[:, :, None, None]
    entry = jnp.sum(weights * block_ends[None], axis=1)
    mixed, _ = run_scan(flags, values, factor, entry, li_residue)
    return mixed.reshape(shard_rows, channels)


def body(
    tokens,
    mr_gain,
    mr_inproj,
    mr_outproj,
    mr_filter,
    li_gain,
    li_inproj,
    li_outproj,
    li_decay,
    li_residue,
    doc_ids,
):
    mr_piece = gather_weights(mr_inproj)
    li_piece = gather_weights(li_inproj)
    mr_columns = outproj_columns(mr_outproj)
    li_columns = outproj_columns(li_outproj)
    query, product = features_in(tokens, mr_gain, mr_piece)
    mixed = short_mix(product, mr_filter, doc_ids)
    stream = features_out(tokens, query, mixed, mr_columns)
    query, product = features_in(stream, li_gain, li_piece)
    return features_out(stream, query, long_mix(product, li_decay, li_residue, doc_ids), li_columns)


def solution(mesh):
    ctx_count, ch_count = mesh.devices.shape
    pair_count = 2 if ch_count % 2 == 0 else 1
    view = jax.sharding.Mesh(
        mesh.devices.reshape(ctx_count, ch_count // pair_count, pair_count), ("ctx",) + CH
    )
    in_specs = (
        P("ctx", CH),
        P(),
        P("ctx", None, CH),
        P(CH, "ctx"),
        P(None, CH),
        P(),
        P("ctx", None, CH),
        P(CH, "ctx"),
        P(None, CH),
        P(None, CH),
        P(),
    )
    out_specs = P("ctx", CH)
    return jax.shard_map(body, mesh=view, in_specs=in_specs, out_specs=out_specs, check_vma=False)
```

```python
import math

import jax
import jax.numpy as jnp
from jax import lax
from jax.experimental import pallas as pl
from jax.experimental.pallas import tpu as pltpu
from jax.sharding import PartitionSpec as P


def extended(value, sides, width):
    for axis, dim in sides:
        count, length = (lax.axis_size(axis), value.shape[dim])
        up = [(i, (i + 1) % count) for i in range(count - 1)]
        down = [(j, i) for i, j in up]
        last = lax.slice_in_dim(value, length - width, length, axis=dim)
        initial = lax.slice_in_dim(value, 0, width, axis=dim)
        before = lax.ppermute(last, axis, up)
        after = lax.ppermute(initial, axis, down)
        value = jnp.concatenate([before, value, after], axis=dim)
    return value


CH = ("z", "yh")


def gather_channels(value):
    pair = lax.all_gather(value, "yh", axis=1, tiled=True)
    return lax.all_gather(pair, "z", axis=1, tiled=True)


def gather_weights(inproj):
    return lax.all_gather(inproj, "ctx", axis=0, tiled=True)


def gather_by_fanout(value):
    count = lax.axis_size("ctx")
    index = lax.axis_index("ctx")
    received = [value] + [
        lax.ppermute(value, "ctx", [(i, i ^ shift) for i in range(count)]) for shift in range(1, count)
    ]
    order = jnp.bitwise_xor(jnp.arange(count), index)
    blocks = jnp.take(jnp.stack(received), order, axis=0)
    return blocks.reshape((count * value.shape[0],) + value.shape[1:])


def features_in(stream, gain, piece):
    whole = gather_channels(stream)
    floats = whole.astype(jnp.float32)
    scaled = lax.rsqrt(jnp.mean(floats * floats, axis=1, keepdims=True) + 1e-06)
    normed = (floats * scaled * gain[None, :]).astype(jnp.bfloat16)
    channels = piece.shape[2]
    flat = piece.reshape(piece.shape[0], 3 * channels)
    joined = jnp.dot(normed, flat, preferred_element_type=jnp.float32).astype(jnp.bfloat16)
    product = (
        joined[:, channels : 2 * channels].astype(jnp.float32)
        * joined[:, 2 * channels :].astype(jnp.float32)
    ).astype(jnp.bfloat16)
    return (joined[:, :channels], product)


def outproj_columns(outproj, gather=None):
    ctx_count, ch_count = (lax.axis_size("ctx"), lax.axis_size(CH))
    assert ctx_count == ch_count
    pairs = [(i * ch_count + c, c * ch_count + i) for i in range(ctx_count) for c in range(ch_count)]
    swapped = lax.ppermute(outproj, ("ctx",) + CH, pairs)
    if gather is not None:
        return gather(swapped)
    return lax.all_gather(swapped, "ctx", axis=0, tiled=True)


def features_out(stream, query, mixed, columns):
    gated = (query.astype(jnp.float32) * mixed).astype(jnp.bfloat16)
    whole = gather_channels(gated)
    rows, width = gated.shape
    groups = whole.shape[1] // width
    parts = jnp.einsum(
        "tgk,gkj->gtj",
        whole.reshape(rows, groups, width),
        columns.reshape(groups, width, columns.shape[1]),
        preferred_element_type=jnp.float32,
    ).astype(jnp.bfloat16)
    summed = jnp.sum(parts.astype(jnp.float32), axis=0)
    return (stream.astype(jnp.float32) + summed).astype(jnp.bfloat16)


def span_layout(shard_rows):
    ctx_count = lax.axis_size("ctx")
    ctx_index = lax.axis_index("ctx")
    span_rows = shard_rows // 2
    span_starts = jnp.stack([ctx_index * span_rows, (2 * ctx_count - 1 - ctx_index) * span_rows])
    positions = span_starts[:, None] + jnp.arange(span_rows)[None, :]
    return (ctx_count, ctx_index, span_rows, span_starts, positions)


def short_mix(product, mr_filter, doc_ids):
    shard_rows, channels = product.shape
    ctx_count, ctx_index, span_rows, span_starts, _ = span_layout(shard_rows)
    tap_count = mr_filter.shape[0]
    reach_rows = tap_count - 1
    halves = product.reshape(2, span_rows, channels)
    tails = jnp.concatenate(
        [halves[1, span_rows - reach_rows :], halves[0, span_rows - reach_rows :]], 0
    )
    framed = extended(tails, (("ctx", 0),), reach_rows)
    before_upper = jnp.where(
        ctx_index == ctx_count - 1, halves[0, span_rows - reach_rows :], framed[3 * reach_rows :]
    )
    lower_window = jnp.concatenate([framed[:reach_rows], halves[0]], 0)
    upper_window = jnp.concatenate([before_upper, halves[1]], 0)
    windows = jnp.stack([lower_window, upper_window]).astype(jnp.float32)
    window_places = span_starts[:, None] - reach_rows + jnp.arange(reach_rows + span_rows)[None, :]
    window_docs = jnp.where(
        window_places >= 0, jnp.take(doc_ids, jnp.clip(window_places, 0, None)), -1
    )
    target_docs = window_docs[:, reach_rows:]
    tap_block = math.gcd(tap_count, 16)

    def tap_group(group_number, running):
        for offset in range(tap_block):
            tap_lag = group_number * tap_block + offset
            source = lax.dynamic_slice_in_dim(windows, reach_rows - tap_lag, span_rows, 1)
            source_docs = lax.dynamic_slice_in_dim(window_docs, reach_rows - tap_lag, span_rows, 1)
            weight = lax.dynamic_slice_in_dim(mr_filter, tap_lag, 1, 0)
            running = (
                running
                + jnp.where((source_docs == target_docs)[:, :, None], source, 0.0) * weight[None]
            )
        return running

    mixed = lax.fori_loop(
        0, tap_count // tap_block, tap_group, jnp.zeros((2, span_rows, channels), jnp.float32)
    )
    return mixed.reshape(shard_rows, channels)


def scan_kernel(flags_ref, x_ref, factor_ref, init_ref, residue_ref, mixed_ref, end_ref):
    halves, span_rows, _ = x_ref.shape
    factor = factor_ref[...]
    residue = residue_ref[...]
    for half in range(halves):

        def step(t, state):
            kept = factor * flags_ref[half * span_rows + t]
            state = kept * state + x_ref[half, pl.ds(t, 1), :]
            mixed_ref[half, pl.ds(t, 1), :] = jnp.sum(residue * state, axis=0, keepdims=True)
            return state

        end_ref[half] = lax.fori_loop(0, span_rows, step, init_ref[half], unroll=8)


def run_scan(flags, values, factor, init, residue):
    halves, span_rows, channels = values.shape
    modes = factor.shape[0]
    vmem = pl.BlockSpec(memory_space=pltpu.VMEM)
    steps = halves * span_rows * modes * channels
    return pl.pallas_call(
        scan_kernel,
        out_shape=(
            jax.ShapeDtypeStruct((halves, span_rows, channels), jnp.float32),
            jax.ShapeDtypeStruct((halves, modes, channels), jnp.float32),
        ),
        in_specs=[pl.BlockSpec(memory_space=pltpu.SMEM), vmem, vmem, vmem, vmem],
        out_specs=(vmem, vmem),
        cost_estimate=pl.CostEstimate(
            flops=5 * steps, transcendentals=0, bytes_accessed=8 * halves * span_rows * channels
        ),
    )(flags, values, factor, init, residue)


def long_mix(product, li_decay, li_residue, doc_ids):
    shard_rows, channels = product.shape
    ctx_count, _, span_rows, span_starts, positions = span_layout(shard_rows)
    modes = li_decay.shape[0]
    own_docs = jnp.take(doc_ids, positions)
    prior_docs = jnp.take(doc_ids, jnp.clip(positions - 1, 0, None))
    flags = ((positions > 0) & (own_docs == prior_docs)).astype(jnp.float32).reshape(-1)
    factor = jnp.exp(-li_decay)
    values = product.reshape(2, span_rows, channels).astype(jnp.float32)
    zeros = jnp.zeros((2, modes, channels), jnp.float32)
    _, ends = run_scan(flags, values, factor, zeros, li_residue)
    gathered = lax.all_gather(ends, "ctx", axis=0, tiled=False)
    block_ends = jnp.concatenate([gathered[:, 0], gathered[::-1, 1]], 0)
    block_count = 2 * ctx_count
    blocks = jnp.arange(block_count)
    end_docs = jnp.take(doc_ids, (blocks + 1) * span_rows - 1)
    targets = span_starts // span_rows
    entry_docs = jnp.take(doc_ids, jnp.clip(span_starts - 1, 0, None))
    linked = (blocks[None, :] < targets[:, None]) & (end_docs[None, :] == entry_docs[:, None])
    distance = jnp.where(linked, (targets[:, None] - blocks[None, :] - 1) * span_rows, 0).astype(jnp.float32)
    weights = jnp.exp(-li_decay[None, None] * distance[:, :, None, None]) * linked.astype(jnp.float32)[:, :, None, None]
    entry = jnp.sum(weights * block_ends[None], axis=1)
    mixed, _ = run_scan(flags, values, factor, entry, li_residue)
    return mixed.reshape(shard_rows, channels)


def body(
    tokens,
    mr_gain,
    mr_inproj,
    mr_outproj,
    mr_filter,
    li_gain,
    li_inproj,
    li_outproj,
    li_decay,
    li_residue,
    doc_ids,
):
    mr_piece = gather_weights(mr_inproj)
    li_piece = gather_by_fanout(li_inproj)
    mr_columns = outproj_columns(mr_outproj)
    li_columns = outproj_columns(li_outproj)
    query, product = features_in(tokens, mr_gain, mr_piece)
    mixed = short_mix(product, mr_filter, doc_ids)
    stream = features_out(tokens, query, mixed, mr_columns)
    query, product = features_in(stream, li_gain, li_piece)
    return features_out(stream, query, long_mix(product, li_decay, li_residue, doc_ids), li_columns)


def solution(mesh):
    ctx_count, ch_count = mesh.devices.shape
    pair_count = 2 if ch_count % 2 == 0 else 1
    view = jax.sharding.Mesh(
        mesh.devices.reshape(ctx_count, ch_count // pair_count, pair_count), ("ctx",) + CH
    )
    in_specs = (
        P("ctx", CH),
        P(),
        P("ctx", None, CH),
        P(CH, "ctx"),
        P(None, CH),
        P(),
        P("ctx", None, CH),
        P(CH, "ctx"),
        P(None, CH),
        P(None, CH),
        P(),
    )
    out_specs = P("ctx", CH)
    return jax.shard_map(body, mesh=view, in_specs=in_specs, out_specs=out_specs, check_vma=False)
```

```python
import math

import jax
import jax.numpy as jnp
from jax import lax
from jax.experimental import pallas as pl
from jax.experimental.pallas import tpu as pltpu
from jax.sharding import PartitionSpec as P


def extended(value, sides, width):
    for axis, dim in sides:
        count, length = (lax.axis_size(axis), value.shape[dim])
        up = [(i, (i + 1) % count) for i in range(count - 1)]
        down = [(j, i) for i, j in up]
        last = lax.slice_in_dim(value, length - width, length, axis=dim)
        initial = lax.slice_in_dim(value, 0, width, axis=dim)
        before = lax.ppermute(last, axis, up)
        after = lax.ppermute(initial, axis, down)
        value = jnp.concatenate([before, value, after], axis=dim)
    return value


CH = ("z", "yh")


def gather_channels(value):
    pair = lax.all_gather(value, "yh", axis=1, tiled=True)
    return lax.all_gather(pair, "z", axis=1, tiled=True)


def gather_weights(inproj):
    return lax.all_gather(inproj, "ctx", axis=0, tiled=True)


def features_in(stream, gain, piece):
    whole = gather_channels(stream)
    floats = whole.astype(jnp.float32)
    scaled = lax.rsqrt(jnp.mean(floats * floats, axis=1, keepdims=True) + 1e-06)
    normed = (floats * scaled * gain[None, :]).astype(jnp.bfloat16)
    channels = piece.shape[2]
    flat = piece.reshape(piece.shape[0], 3 * channels)
    joined = jnp.dot(normed, flat, preferred_element_type=jnp.float32).astype(jnp.bfloat16)
    product = (
        joined[:, channels : 2 * channels].astype(jnp.float32)
        * joined[:, 2 * channels :].astype(jnp.float32)
    ).astype(jnp.bfloat16)
    return (joined[:, :channels], product)


def swap_blocks(outproj):
    ctx_count, ch_count = (lax.axis_size("ctx"), lax.axis_size(CH))
    assert ctx_count == ch_count
    pairs = [(i * ch_count + c, c * ch_count + i) for i in range(ctx_count) for c in range(ch_count)]
    return lax.ppermute(outproj, ("ctx",) + CH, pairs)


def outproj_columns(outproj):
    return lax.all_gather(swap_blocks(outproj), "ctx", axis=0, tiled=True)


def gather_layer_weights(inproj, outproj):
    rows, parts, channels = inproj.shape
    joined = jnp.concatenate([inproj.reshape(rows, parts * channels), swap_blocks(outproj)], 1)
    whole = lax.all_gather(joined, "ctx", axis=0, tiled=True)
    piece = whole[:, : parts * channels].reshape(whole.shape[0], parts, channels)
    return piece, whole[:, parts * channels :]


def features_out(stream, query, mixed, columns):
    gated = (query.astype(jnp.float32) * mixed).astype(jnp.bfloat16)
    whole = gather_channels(gated)
    rows, width = gated.shape
    groups = whole.shape[1] // width
    parts = jnp.einsum(
        "tgk,gkj->gtj",
        whole.reshape(rows, groups, width),
        columns.reshape(groups, width, columns.shape[1]),
        preferred_element_type=jnp.float32,
    ).astype(jnp.bfloat16)
    summed = jnp.sum(parts.astype(jnp.float32), axis=0)
    return (stream.astype(jnp.float32) + summed).astype(jnp.bfloat16)


def span_layout(shard_rows):
    ctx_count = lax.axis_size("ctx")
    ctx_index = lax.axis_index("ctx")
    span_rows = shard_rows // 2
    span_starts = jnp.stack([ctx_index * span_rows, (2 * ctx_count - 1 - ctx_index) * span_rows])
    positions = span_starts[:, None] + jnp.arange(span_rows)[None, :]
    return (ctx_count, ctx_index, span_rows, span_starts, positions)


def short_mix(product, mr_filter, doc_ids):
    shard_rows, channels = product.shape
    ctx_count, ctx_index, span_rows, span_starts, _ = span_layout(shard_rows)
    tap_count = mr_filter.shape[0]
    reach_rows = tap_count - 1
    halves = product.reshape(2, span_rows, channels)
    tails = jnp.concatenate(
        [halves[1, span_rows - reach_rows :], halves[0, span_rows - reach_rows :]], 0
    )
    framed = extended(tails, (("ctx", 0),), reach_rows)
    before_upper = jnp.where(
        ctx_index == ctx_count - 1, halves[0, span_rows - reach_rows :], framed[3 * reach_rows :]
    )
    lower_window = jnp.concatenate([framed[:reach_rows], halves[0]], 0)
    upper_window = jnp.concatenate([before_upper, halves[1]], 0)
    windows = jnp.stack([lower_window, upper_window]).astype(jnp.float32)
    window_places = span_starts[:, None] - reach_rows + jnp.arange(reach_rows + span_rows)[None, :]
    window_docs = jnp.where(
        window_places >= 0, jnp.take(doc_ids, jnp.clip(window_places, 0, None)), -1
    )
    target_docs = window_docs[:, reach_rows:]
    tap_block = math.gcd(tap_count, 16)

    def tap_group(group_number, running):
        for offset in range(tap_block):
            tap_lag = group_number * tap_block + offset
            source = lax.dynamic_slice_in_dim(windows, reach_rows - tap_lag, span_rows, 1)
            source_docs = lax.dynamic_slice_in_dim(window_docs, reach_rows - tap_lag, span_rows, 1)
            weight = lax.dynamic_slice_in_dim(mr_filter, tap_lag, 1, 0)
            running = (
                running
                + jnp.where((source_docs == target_docs)[:, :, None], source, 0.0) * weight[None]
            )
        return running

    mixed = lax.fori_loop(
        0, tap_count // tap_block, tap_group, jnp.zeros((2, span_rows, channels), jnp.float32)
    )
    return mixed.reshape(shard_rows, channels)


def scan_kernel(flags_ref, x_ref, factor_ref, init_ref, residue_ref, mixed_ref, end_ref):
    halves, span_rows, _ = x_ref.shape
    factor = factor_ref[...]
    residue = residue_ref[...]
    for half in range(halves):

        def step(t, state):
            kept = factor * flags_ref[half * span_rows + t]
            state = kept * state + x_ref[half, pl.ds(t, 1), :]
            mixed_ref[half, pl.ds(t, 1), :] = jnp.sum(residue * state, axis=0, keepdims=True)
            return state

        end_ref[half] = lax.fori_loop(0, span_rows, step, init_ref[half], unroll=8)


def run_scan(flags, values, factor, init, residue):
    halves, span_rows, channels = values.shape
    modes = factor.shape[0]
    vmem = pl.BlockSpec(memory_space=pltpu.VMEM)
    steps = halves * span_rows * modes * channels
    return pl.pallas_call(
        scan_kernel,
        out_shape=(
            jax.ShapeDtypeStruct((halves, span_rows, channels), jnp.float32),
            jax.ShapeDtypeStruct((halves, modes, channels), jnp.float32),
        ),
        in_specs=[pl.BlockSpec(memory_space=pltpu.SMEM), vmem, vmem, vmem, vmem],
        out_specs=(vmem, vmem),
        cost_estimate=pl.CostEstimate(
            flops=5 * steps, transcendentals=0, bytes_accessed=8 * halves * span_rows * channels
        ),
    )(flags, values, factor, init, residue)


def long_mix(product, li_decay, li_residue, doc_ids):
    shard_rows, channels = product.shape
    ctx_count, _, span_rows, span_starts, positions = span_layout(shard_rows)
    modes = li_decay.shape[0]
    own_docs = jnp.take(doc_ids, positions)
    prior_docs = jnp.take(doc_ids, jnp.clip(positions - 1, 0, None))
    flags = ((positions > 0) & (own_docs == prior_docs)).astype(jnp.float32).reshape(-1)
    factor = jnp.exp(-li_decay)
    values = product.reshape(2, span_rows, channels).astype(jnp.float32)
    zeros = jnp.zeros((2, modes, channels), jnp.float32)
    _, ends = run_scan(flags, values, factor, zeros, li_residue)
    gathered = lax.all_gather(ends, "ctx", axis=0, tiled=False)
    block_ends = jnp.concatenate([gathered[:, 0], gathered[::-1, 1]], 0)
    block_count = 2 * ctx_count
    blocks = jnp.arange(block_count)
    end_docs = jnp.take(doc_ids, (blocks + 1) * span_rows - 1)
    targets = span_starts // span_rows
    entry_docs = jnp.take(doc_ids, jnp.clip(span_starts - 1, 0, None))
    linked = (blocks[None, :] < targets[:, None]) & (end_docs[None, :] == entry_docs[:, None])
    distance = jnp.where(linked, (targets[:, None] - blocks[None, :] - 1) * span_rows, 0).astype(jnp.float32)
    weights = jnp.exp(-li_decay[None, None] * distance[:, :, None, None]) * linked.astype(jnp.float32)[:, :, None, None]
    entry = jnp.sum(weights * block_ends[None], axis=1)
    mixed, _ = run_scan(flags, values, factor, entry, li_residue)
    return mixed.reshape(shard_rows, channels)


def body(
    tokens,
    mr_gain,
    mr_inproj,
    mr_outproj,
    mr_filter,
    li_gain,
    li_inproj,
    li_outproj,
    li_decay,
    li_residue,
    doc_ids,
):
    mr_piece, mr_columns = gather_layer_weights(mr_inproj, mr_outproj)
    li_piece = gather_weights(li_inproj)
    li_columns = outproj_columns(li_outproj)
    query, product = features_in(tokens, mr_gain, mr_piece)
    mixed = short_mix(product, mr_filter, doc_ids)
    stream = features_out(tokens, query, mixed, mr_columns)
    query, product = features_in(stream, li_gain, li_piece)
    return features_out(stream, query, long_mix(product, li_decay, li_residue, doc_ids), li_columns)


def solution(mesh):
    ctx_count, ch_count = mesh.devices.shape
    pair_count = 2 if ch_count % 2 == 0 else 1
    view = jax.sharding.Mesh(
        mesh.devices.reshape(ctx_count, ch_count // pair_count, pair_count), ("ctx",) + CH
    )
    in_specs = (
        P("ctx", CH),
        P(),
        P("ctx", None, CH),
        P(CH, "ctx"),
        P(None, CH),
        P(),
        P("ctx", None, CH),
        P(CH, "ctx"),
        P(None, CH),
        P(None, CH),
        P(),
    )
    out_specs = P("ctx", CH)
    return jax.shard_map(body, mesh=view, in_specs=in_specs, out_specs=out_specs, check_vma=False)
```

```python
import math

import jax
import jax.numpy as jnp
from jax import lax
from jax.experimental import pallas as pl
from jax.experimental.pallas import tpu as pltpu
from jax.sharding import PartitionSpec as P


def extended(value, sides, width):
    for axis, dim in sides:
        count, length = (lax.axis_size(axis), value.shape[dim])
        up = [(i, (i + 1) % count) for i in range(count - 1)]
        down = [(j, i) for i, j in up]
        last = lax.slice_in_dim(value, length - width, length, axis=dim)
        initial = lax.slice_in_dim(value, 0, width, axis=dim)
        before = lax.ppermute(last, axis, up)
        after = lax.ppermute(initial, axis, down)
        value = jnp.concatenate([before, value, after], axis=dim)
    return value


CH = ("z", "yh")


def gather_channels(value):
    pair = lax.all_gather(value, "yh", axis=1, tiled=True)
    return lax.all_gather(pair, "z", axis=1, tiled=True)


def gather_weights(inproj):
    return lax.all_gather(inproj, "ctx", axis=0, tiled=True)


def features_in(stream, gain, piece):
    whole = gather_channels(stream)
    floats = whole.astype(jnp.float32)
    scaled = lax.rsqrt(jnp.mean(floats * floats, axis=1, keepdims=True) + 1e-06)
    normed = (floats * scaled * gain[None, :]).astype(jnp.bfloat16)
    channels = piece.shape[2]
    flat = piece.reshape(piece.shape[0], 3 * channels)
    joined = jnp.dot(normed, flat, preferred_element_type=jnp.float32).astype(jnp.bfloat16)
    product = (
        joined[:, channels : 2 * channels].astype(jnp.float32)
        * joined[:, 2 * channels :].astype(jnp.float32)
    ).astype(jnp.bfloat16)
    return (joined[:, :channels], product)


def swap_blocks(outproj):
    ctx_count, ch_count = (lax.axis_size("ctx"), lax.axis_size(CH))
    assert ctx_count == ch_count
    pairs = [(i * ch_count + c, c * ch_count + i) for i in range(ctx_count) for c in range(ch_count)]
    return lax.ppermute(outproj, ("ctx",) + CH, pairs)


def outproj_columns(outproj):
    return lax.all_gather(swap_blocks(outproj), "ctx", axis=0, tiled=True)


def gather_layer_weights(inproj, outproj):
    rows, parts, channels = inproj.shape
    joined = jnp.concatenate([inproj.reshape(rows, parts * channels), swap_blocks(outproj)], 1)
    whole = lax.all_gather(joined, "ctx", axis=0, tiled=True)
    piece = whole[:, : parts * channels].reshape(whole.shape[0], parts, channels)
    return piece, whole[:, parts * channels :]


def features_out(stream, query, mixed, columns):
    gated = (query.astype(jnp.float32) * mixed).astype(jnp.bfloat16)
    whole = gather_channels(gated)
    rows, width = gated.shape
    groups = whole.shape[1] // width
    parts = jnp.einsum(
        "tgk,gkj->gtj",
        whole.reshape(rows, groups, width),
        columns.reshape(groups, width, columns.shape[1]),
        preferred_element_type=jnp.bfloat16,
    )
    summed = jnp.sum(parts.astype(jnp.float32), axis=0)
    return (stream.astype(jnp.float32) + summed).astype(jnp.bfloat16)


def span_layout(shard_rows):
    ctx_count = lax.axis_size("ctx")
    ctx_index = lax.axis_index("ctx")
    span_rows = shard_rows // 2
    span_starts = jnp.stack([ctx_index * span_rows, (2 * ctx_count - 1 - ctx_index) * span_rows])
    positions = span_starts[:, None] + jnp.arange(span_rows)[None, :]
    return (ctx_count, ctx_index, span_rows, span_starts, positions)


def short_mix(product, mr_filter, doc_ids):
    shard_rows, channels = product.shape
    ctx_count, ctx_index, span_rows, span_starts, _ = span_layout(shard_rows)
    tap_count = mr_filter.shape[0]
    reach_rows = tap_count - 1
    halves = product.reshape(2, span_rows, channels)
    tails = jnp.concatenate(
        [halves[1, span_rows - reach_rows :], halves[0, span_rows - reach_rows :]], 0
    )
    framed = extended(tails, (("ctx", 0),), reach_rows)
    before_upper = jnp.where(
        ctx_index == ctx_count - 1, halves[0, span_rows - reach_rows :], framed[3 * reach_rows :]
    )
    lower_window = jnp.concatenate([framed[:reach_rows], halves[0]], 0)
    upper_window = jnp.concatenate([before_upper, halves[1]], 0)
    windows = jnp.stack([lower_window, upper_window]).astype(jnp.float32)
    window_places = span_starts[:, None] - reach_rows + jnp.arange(reach_rows + span_rows)[None, :]
    window_docs = jnp.where(
        window_places >= 0, jnp.take(doc_ids, jnp.clip(window_places, 0, None)), -1
    )
    target_docs = window_docs[:, reach_rows:]
    tap_block = math.gcd(tap_count, 16)

    def tap_group(group_number, running):
        for offset in range(tap_block):
            tap_lag = group_number * tap_block + offset
            source = lax.dynamic_slice_in_dim(windows, reach_rows - tap_lag, span_rows, 1)
            source_docs = lax.dynamic_slice_in_dim(window_docs, reach_rows - tap_lag, span_rows, 1)
            weight = lax.dynamic_slice_in_dim(mr_filter, tap_lag, 1, 0)
            running = (
                running
                + jnp.where((source_docs == target_docs)[:, :, None], source, 0.0) * weight[None]
            )
        return running

    mixed = lax.fori_loop(
        0, tap_count // tap_block, tap_group, jnp.zeros((2, span_rows, channels), jnp.float32)
    )
    return mixed.reshape(shard_rows, channels)


def scan_kernel(flags_ref, x_ref, factor_ref, init_ref, residue_ref, mixed_ref, end_ref):
    halves, span_rows, _ = x_ref.shape
    factor = factor_ref[...]
    residue = residue_ref[...]
    for half in range(halves):

        def step(t, state):
            kept = factor * flags_ref[half * span_rows + t]
            state = kept * state + x_ref[half, pl.ds(t, 1), :]
            mixed_ref[half, pl.ds(t, 1), :] = jnp.sum(residue * state, axis=0, keepdims=True)
            return state

        end_ref[half] = lax.fori_loop(0, span_rows, step, init_ref[half], unroll=8)


def run_scan(flags, values, factor, init, residue):
    halves, span_rows, channels = values.shape
    modes = factor.shape[0]
    vmem = pl.BlockSpec(memory_space=pltpu.VMEM)
    steps = halves * span_rows * modes * channels
    return pl.pallas_call(
        scan_kernel,
        out_shape=(
            jax.ShapeDtypeStruct((halves, span_rows, channels), jnp.float32),
            jax.ShapeDtypeStruct((halves, modes, channels), jnp.float32),
        ),
        in_specs=[pl.BlockSpec(memory_space=pltpu.SMEM), vmem, vmem, vmem, vmem],
        out_specs=(vmem, vmem),
        cost_estimate=pl.CostEstimate(
            flops=5 * steps, transcendentals=0, bytes_accessed=8 * halves * span_rows * channels
        ),
    )(flags, values, factor, init, residue)


def li_tables(doc_ids, li_decay, shard_rows):
    ctx_count, _, span_rows, span_starts, positions = span_layout(shard_rows)
    own_docs = jnp.stack([lax.dynamic_slice_in_dim(doc_ids, start, span_rows) for start in span_starts])
    padded = jnp.concatenate([doc_ids[:1], doc_ids])
    prior_docs = jnp.stack([lax.dynamic_slice_in_dim(padded, start, span_rows) for start in span_starts])
    flags = ((positions > 0) & (own_docs == prior_docs)).astype(jnp.float32).reshape(-1)
    block_count = 2 * ctx_count
    blocks = jnp.arange(block_count)
    end_docs = jnp.take(doc_ids, (blocks + 1) * span_rows - 1)
    targets = span_starts // span_rows
    entry_docs = jnp.take(doc_ids, jnp.clip(span_starts - 1, 0, None))
    linked = (blocks[None, :] < targets[:, None]) & (end_docs[None, :] == entry_docs[:, None])
    distance = jnp.where(linked, (targets[:, None] - blocks[None, :] - 1) * span_rows, 0).astype(jnp.float32)
    weights = jnp.exp(-li_decay[None, None] * distance[:, :, None, None]) * linked.astype(jnp.float32)[:, :, None, None]
    return flags, weights


def long_mix(product, li_decay, li_residue, tables):
    flags, weights = tables
    shard_rows, channels = product.shape
    span_rows = shard_rows // 2
    modes = li_decay.shape[0]
    factor = jnp.exp(-li_decay)
    values = product.reshape(2, span_rows, channels).astype(jnp.float32)
    zeros = jnp.zeros((2, modes, channels), jnp.float32)
    _, ends = run_scan(flags, values, factor, zeros, li_residue)
    gathered = lax.all_gather(ends, "ctx", axis=0, tiled=False)
    block_ends = jnp.concatenate([gathered[:, 0], gathered[::-1, 1]], 0)
    entry = jnp.sum(weights * block_ends[None], axis=1)
    mixed, _ = run_scan(flags, values, factor, entry, li_residue)
    return mixed.reshape(shard_rows, channels)


def body(
    tokens,
    mr_gain,
    mr_inproj,
    mr_outproj,
    mr_filter,
    li_gain,
    li_inproj,
    li_outproj,
    li_decay,
    li_residue,
    doc_ids,
):
    mr_piece, mr_columns = gather_layer_weights(mr_inproj, mr_outproj)
    li_piece = gather_weights(li_inproj)
    tables = li_tables(doc_ids, li_decay, tokens.shape[0])
    li_columns = outproj_columns(li_outproj)
    query, product = features_in(tokens, mr_gain, mr_piece)
    mixed = short_mix(product, mr_filter, doc_ids)
    stream = features_out(tokens, query, mixed, mr_columns)
    query, product = features_in(stream, li_gain, li_piece)
    return features_out(stream, query, long_mix(product, li_decay, li_residue, tables), li_columns)


def solution(mesh):
    ctx_count, ch_count = mesh.devices.shape
    pair_count = 2 if ch_count % 2 == 0 else 1
    view = jax.sharding.Mesh(
        mesh.devices.reshape(ctx_count, ch_count // pair_count, pair_count), ("ctx",) + CH
    )
    in_specs = (
        P("ctx", CH),
        P(),
        P("ctx", None, CH),
        P(CH, "ctx"),
        P(None, CH),
        P(),
        P("ctx", None, CH),
        P(CH, "ctx"),
        P(None, CH),
        P(None, CH),
        P(),
    )
    out_specs = P("ctx", CH)
    return jax.shard_map(body, mesh=view, in_specs=in_specs, out_specs=out_specs, check_vma=False)
```

```python
import math

import jax
import jax.numpy as jnp
from jax import lax
from jax.experimental import pallas as pl
from jax.experimental.pallas import tpu as pltpu
from jax.sharding import PartitionSpec as P


def extended(value, sides, width):
    for axis, dim in sides:
        count, length = (lax.axis_size(axis), value.shape[dim])
        up = [(i, (i + 1) % count) for i in range(count - 1)]
        down = [(j, i) for i, j in up]
        last = lax.slice_in_dim(value, length - width, length, axis=dim)
        initial = lax.slice_in_dim(value, 0, width, axis=dim)
        before = lax.ppermute(last, axis, up)
        after = lax.ppermute(initial, axis, down)
        value = jnp.concatenate([before, value, after], axis=dim)
    return value


CH = ("z", "yh")


def gather_channels(value):
    pair = lax.all_gather(value, "yh", axis=1, tiled=True)
    return lax.all_gather(pair, "z", axis=1, tiled=True)


def gather_weights(inproj):
    return lax.all_gather(inproj, "ctx", axis=0, tiled=True)


def features_in(stream, gain, piece):
    whole = gather_channels(stream)
    floats = whole.astype(jnp.float32)
    scaled = lax.rsqrt(jnp.mean(floats * floats, axis=1, keepdims=True) + 1e-06)
    normed = (floats * scaled * gain[None, :]).astype(jnp.bfloat16)
    channels = piece.shape[2]
    flat = piece.reshape(piece.shape[0], 3 * channels)
    joined = jnp.dot(normed, flat, preferred_element_type=jnp.float32).astype(jnp.bfloat16)
    product = (
        joined[:, channels : 2 * channels].astype(jnp.float32)
        * joined[:, 2 * channels :].astype(jnp.float32)
    ).astype(jnp.bfloat16)
    return (joined[:, :channels], product)


def swap_blocks(outproj):
    ctx_count, ch_count = (lax.axis_size("ctx"), lax.axis_size(CH))
    assert ctx_count == ch_count
    pairs = [(i * ch_count + c, c * ch_count + i) for i in range(ctx_count) for c in range(ch_count)]
    return lax.ppermute(outproj, ("ctx",) + CH, pairs)


def outproj_columns(outproj):
    return lax.all_gather(swap_blocks(outproj), "ctx", axis=0, tiled=True)


def gather_layer_weights(inproj, outproj):
    rows, parts, channels = inproj.shape
    joined = jnp.concatenate([inproj.reshape(rows, parts * channels), swap_blocks(outproj)], 1)
    whole = lax.all_gather(joined, "ctx", axis=0, tiled=True)
    piece = whole[:, : parts * channels].reshape(whole.shape[0], parts, channels)
    return piece, whole[:, parts * channels :]


def features_out(stream, query, mixed, columns):
    gated = (query.astype(jnp.float32) * mixed).astype(jnp.bfloat16)
    whole = gather_channels(gated)
    rows, width = gated.shape
    groups = whole.shape[1] // width
    parts = jnp.einsum(
        "tgk,gkj->gtj",
        whole.reshape(rows, groups, width),
        columns.reshape(groups, width, columns.shape[1]),
        preferred_element_type=jnp.bfloat16,
    )
    summed = jnp.sum(parts.astype(jnp.float32), axis=0)
    return (stream.astype(jnp.float32) + summed).astype(jnp.bfloat16)


def span_layout(shard_rows):
    ctx_count = lax.axis_size("ctx")
    ctx_index = lax.axis_index("ctx")
    span_rows = shard_rows // 2
    span_starts = jnp.stack([ctx_index * span_rows, (2 * ctx_count - 1 - ctx_index) * span_rows])
    positions = span_starts[:, None] + jnp.arange(span_rows)[None, :]
    return (ctx_count, ctx_index, span_rows, span_starts, positions)


def short_mix(product, mr_filter, doc_ids):
    shard_rows, channels = product.shape
    ctx_count, ctx_index, span_rows, span_starts, _ = span_layout(shard_rows)
    tap_count = mr_filter.shape[0]
    reach_rows = tap_count - 1
    halves = product.reshape(2, span_rows, channels)
    tails = jnp.concatenate(
        [halves[1, span_rows - reach_rows :], halves[0, span_rows - reach_rows :]], 0
    )
    framed = extended(tails, (("ctx", 0),), reach_rows)
    before_upper = jnp.where(
        ctx_index == ctx_count - 1, halves[0, span_rows - reach_rows :], framed[3 * reach_rows :]
    )
    lower_window = jnp.concatenate([framed[:reach_rows], halves[0]], 0)
    upper_window = jnp.concatenate([before_upper, halves[1]], 0)
    windows = jnp.stack([lower_window, upper_window]).astype(jnp.float32)
    window_places = span_starts[:, None] - reach_rows + jnp.arange(reach_rows + span_rows)[None, :]
    window_docs = jnp.where(
        window_places >= 0, jnp.take(doc_ids, jnp.clip(window_places, 0, None)), -1
    )
    target_docs = window_docs[:, reach_rows:]
    tap_block = math.gcd(tap_count, 16)

    def tap_group(group_number, running):
        for offset in range(tap_block):
            tap_lag = group_number * tap_block + offset
            source = lax.dynamic_slice_in_dim(windows, reach_rows - tap_lag, span_rows, 1)
            source_docs = lax.dynamic_slice_in_dim(window_docs, reach_rows - tap_lag, span_rows, 1)
            weight = lax.dynamic_slice_in_dim(mr_filter, tap_lag, 1, 0)
            running = (
                running
                + jnp.where((source_docs == target_docs)[:, :, None], source, 0.0) * weight[None]
            )
        return running

    mixed = lax.fori_loop(
        0, tap_count // tap_block, tap_group, jnp.zeros((2, span_rows, channels), jnp.float32)
    )
    return mixed.reshape(shard_rows, channels)


def scan_kernel(flags_ref, x_ref, factor_ref, init_ref, residue_ref, mixed_ref, end_ref):
    halves, span_rows, _ = x_ref.shape
    factor = factor_ref[...]
    residue = residue_ref[...]

    def step(t, states):
        updated = []
        for half in range(halves):
            kept = factor * flags_ref[half * span_rows + t]
            state = kept * states[half] + x_ref[half, pl.ds(t, 1), :]
            mixed_ref[half, pl.ds(t, 1), :] = jnp.sum(residue * state, axis=0, keepdims=True)
            updated.append(state)
        return tuple(updated)

    ends = lax.fori_loop(0, span_rows, step, tuple(init_ref[half] for half in range(halves)), unroll=8)
    for half in range(halves):
        end_ref[half] = ends[half]


def run_scan(flags, values, factor, init, residue):
    halves, span_rows, channels = values.shape
    modes = factor.shape[0]
    vmem = pl.BlockSpec(memory_space=pltpu.VMEM)
    steps = halves * span_rows * modes * channels
    return pl.pallas_call(
        scan_kernel,
        out_shape=(
            jax.ShapeDtypeStruct((halves, span_rows, channels), jnp.float32),
            jax.ShapeDtypeStruct((halves, modes, channels), jnp.float32),
        ),
        in_specs=[pl.BlockSpec(memory_space=pltpu.SMEM), vmem, vmem, vmem, vmem],
        out_specs=(vmem, vmem),
        cost_estimate=pl.CostEstimate(
            flops=5 * steps, transcendentals=0, bytes_accessed=8 * halves * span_rows * channels
        ),
    )(flags, values, factor, init, residue)


def li_tables(doc_ids, li_decay, shard_rows):
    ctx_count, _, span_rows, span_starts, positions = span_layout(shard_rows)
    own_docs = jnp.stack([lax.dynamic_slice_in_dim(doc_ids, start, span_rows) for start in span_starts])
    padded = jnp.concatenate([doc_ids[:1], doc_ids])
    prior_docs = jnp.stack([lax.dynamic_slice_in_dim(padded, start, span_rows) for start in span_starts])
    flags = ((positions > 0) & (own_docs == prior_docs)).astype(jnp.float32).reshape(-1)
    block_count = 2 * ctx_count
    blocks = jnp.arange(block_count)
    end_docs = jnp.take(doc_ids, (blocks + 1) * span_rows - 1)
    targets = span_starts // span_rows
    entry_docs = jnp.take(doc_ids, jnp.clip(span_starts - 1, 0, None))
    linked = (blocks[None, :] < targets[:, None]) & (end_docs[None, :] == entry_docs[:, None])
    distance = jnp.where(linked, (targets[:, None] - blocks[None, :] - 1) * span_rows, 0).astype(jnp.float32)
    weights = jnp.exp(-li_decay[None, None] * distance[:, :, None, None]) * linked.astype(jnp.float32)[:, :, None, None]
    return flags, weights


def long_mix(product, li_decay, li_residue, tables):
    flags, weights = tables
    shard_rows, channels = product.shape
    span_rows = shard_rows // 2
    modes = li_decay.shape[0]
    factor = jnp.exp(-li_decay)
    values = product.reshape(2, span_rows, channels).astype(jnp.float32)
    zeros = jnp.zeros((2, modes, channels), jnp.float32)
    _, ends = run_scan(flags, values, factor, zeros, li_residue)
    gathered = lax.all_gather(ends, "ctx", axis=0, tiled=False)
    block_ends = jnp.concatenate([gathered[:, 0], gathered[::-1, 1]], 0)
    entry = jnp.sum(weights * block_ends[None], axis=1)
    mixed, _ = run_scan(flags, values, factor, entry, li_residue)
    return mixed.reshape(shard_rows, channels)


def body(
    tokens,
    mr_gain,
    mr_inproj,
    mr_outproj,
    mr_filter,
    li_gain,
    li_inproj,
    li_outproj,
    li_decay,
    li_residue,
    doc_ids,
):
    mr_piece, mr_columns = gather_layer_weights(mr_inproj, mr_outproj)
    li_piece = gather_weights(li_inproj)
    tables = li_tables(doc_ids, li_decay, tokens.shape[0])
    li_columns = outproj_columns(li_outproj)
    query, product = features_in(tokens, mr_gain, mr_piece)
    mixed = short_mix(product, mr_filter, doc_ids)
    stream = features_out(tokens, query, mixed, mr_columns)
    query, product = features_in(stream, li_gain, li_piece)
    return features_out(stream, query, long_mix(product, li_decay, li_residue, tables), li_columns)


def solution(mesh):
    ctx_count, ch_count = mesh.devices.shape
    pair_count = 2 if ch_count % 2 == 0 else 1
    view = jax.sharding.Mesh(
        mesh.devices.reshape(ctx_count, ch_count // pair_count, pair_count), ("ctx",) + CH
    )
    in_specs = (
        P("ctx", CH),
        P(),
        P("ctx", None, CH),
        P(CH, "ctx"),
        P(None, CH),
        P(),
        P("ctx", None, CH),
        P(CH, "ctx"),
        P(None, CH),
        P(None, CH),
        P(),
    )
    out_specs = P("ctx", CH)
    return jax.shard_map(body, mesh=view, in_specs=in_specs, out_specs=out_specs, check_vma=False)
```

```python
import math

import jax
import jax.numpy as jnp
from jax import lax
from jax.experimental import pallas as pl
from jax.experimental.pallas import tpu as pltpu
from jax.sharding import PartitionSpec as P


def extended(value, sides, width):
    for axis, dim in sides:
        count, length = (lax.axis_size(axis), value.shape[dim])
        up = [(i, (i + 1) % count) for i in range(count - 1)]
        down = [(j, i) for i, j in up]
        last = lax.slice_in_dim(value, length - width, length, axis=dim)
        initial = lax.slice_in_dim(value, 0, width, axis=dim)
        before = lax.ppermute(last, axis, up)
        after = lax.ppermute(initial, axis, down)
        value = jnp.concatenate([before, value, after], axis=dim)
    return value


CH = ("z", "yh")


def gather_channels(value):
    pair = lax.all_gather(value, "yh", axis=1, tiled=True)
    return lax.all_gather(pair, "z", axis=1, tiled=True)


def gather_weights(inproj):
    return lax.all_gather(inproj, "ctx", axis=0, tiled=True)


def features_in(stream, gain, piece):
    whole = gather_channels(stream)
    floats = whole.astype(jnp.float32)
    scaled = lax.rsqrt(jnp.mean(floats * floats, axis=1, keepdims=True) + 1e-06)
    normed = (floats * scaled * gain[None, :]).astype(jnp.bfloat16)
    channels = piece.shape[2]
    flat = piece.reshape(piece.shape[0], 3 * channels)
    joined = jnp.dot(normed, flat, preferred_element_type=jnp.float32).astype(jnp.bfloat16)
    product = (
        joined[:, channels : 2 * channels].astype(jnp.float32)
        * joined[:, 2 * channels :].astype(jnp.float32)
    ).astype(jnp.bfloat16)
    return (joined[:, :channels], product)


def swap_blocks(outproj):
    ctx_count, ch_count = (lax.axis_size("ctx"), lax.axis_size(CH))
    assert ctx_count == ch_count
    pairs = [(i * ch_count + c, c * ch_count + i) for i in range(ctx_count) for c in range(ch_count)]
    return lax.ppermute(outproj, ("ctx",) + CH, pairs)


def outproj_columns(outproj):
    return lax.all_gather(swap_blocks(outproj), "ctx", axis=0, tiled=True)


def gather_layer_weights(inproj, outproj):
    rows, parts, channels = inproj.shape
    joined = jnp.concatenate([inproj.reshape(rows, parts * channels), swap_blocks(outproj)], 1)
    whole = lax.all_gather(joined, "ctx", axis=0, tiled=True)
    piece = whole[:, : parts * channels].reshape(whole.shape[0], parts, channels)
    return piece, whole[:, parts * channels :]


def outproj_kernel(whole_ref, columns_ref, stream_ref, out_ref):
    width = columns_ref.shape[1]
    groups = whole_ref.shape[1] // width
    summed = None
    for group in range(groups):
        part = jnp.dot(
            whole_ref[:, group * width : (group + 1) * width],
            columns_ref[group * width : (group + 1) * width, :],
            preferred_element_type=jnp.float32,
        ).astype(jnp.bfloat16).astype(jnp.float32)
        summed = part if summed is None else summed + part
    out_ref[...] = (stream_ref[...].astype(jnp.float32) + summed).astype(jnp.bfloat16)


def project_groups(whole, columns, stream):
    vmem = pl.BlockSpec(memory_space=pltpu.VMEM)
    rows, depth = whole.shape
    return pl.pallas_call(
        outproj_kernel,
        out_shape=jax.ShapeDtypeStruct(stream.shape, jnp.bfloat16),
        in_specs=[vmem, vmem, vmem],
        out_specs=vmem,
        cost_estimate=pl.CostEstimate(
            flops=2 * rows * depth * columns.shape[1],
            transcendentals=0,
            bytes_accessed=2 * (whole.size + columns.size + 2 * stream.size),
        ),
    )(whole, columns, stream)


def features_out(stream, query, mixed, columns):
    gated = (query.astype(jnp.float32) * mixed).astype(jnp.bfloat16)
    whole = gather_channels(gated)
    return project_groups(whole, columns, stream)


def span_layout(shard_rows):
    ctx_count = lax.axis_size("ctx")
    ctx_index = lax.axis_index("ctx")
    span_rows = shard_rows // 2
    span_starts = jnp.stack([ctx_index * span_rows, (2 * ctx_count - 1 - ctx_index) * span_rows])
    positions = span_starts[:, None] + jnp.arange(span_rows)[None, :]
    return (ctx_count, ctx_index, span_rows, span_starts, positions)


def short_mix(product, mr_filter, doc_ids):
    shard_rows, channels = product.shape
    ctx_count, ctx_index, span_rows, span_starts, _ = span_layout(shard_rows)
    tap_count = mr_filter.shape[0]
    reach_rows = tap_count - 1
    halves = product.reshape(2, span_rows, channels)
    tails = jnp.concatenate(
        [halves[1, span_rows - reach_rows :], halves[0, span_rows - reach_rows :]], 0
    )
    framed = extended(tails, (("ctx", 0),), reach_rows)
    before_upper = jnp.where(
        ctx_index == ctx_count - 1, halves[0, span_rows - reach_rows :], framed[3 * reach_rows :]
    )
    lower_window = jnp.concatenate([framed[:reach_rows], halves[0]], 0)
    upper_window = jnp.concatenate([before_upper, halves[1]], 0)
    windows = jnp.stack([lower_window, upper_window]).astype(jnp.float32)
    window_places = span_starts[:, None] - reach_rows + jnp.arange(reach_rows + span_rows)[None, :]
    window_docs = jnp.where(
        window_places >= 0, jnp.take(doc_ids, jnp.clip(window_places, 0, None)), -1
    )
    target_docs = window_docs[:, reach_rows:]
    tap_block = math.gcd(tap_count, 16)

    def tap_group(group_number, running):
        for offset in range(tap_block):
            tap_lag = group_number * tap_block + offset
            source = lax.dynamic_slice_in_dim(windows, reach_rows - tap_lag, span_rows, 1)
            source_docs = lax.dynamic_slice_in_dim(window_docs, reach_rows - tap_lag, span_rows, 1)
            weight = lax.dynamic_slice_in_dim(mr_filter, tap_lag, 1, 0)
            running = (
                running
                + jnp.where((source_docs == target_docs)[:, :, None], source, 0.0) * weight[None]
            )
        return running

    mixed = lax.fori_loop(
        0, tap_count // tap_block, tap_group, jnp.zeros((2, span_rows, channels), jnp.float32)
    )
    return mixed.reshape(shard_rows, channels)


def scan_kernel(flags_ref, x_ref, factor_ref, init_ref, residue_ref, mixed_ref, end_ref):
    halves, span_rows, _ = x_ref.shape
    factor = factor_ref[...]
    residue = residue_ref[...]

    def step(t, states):
        updated = []
        for half in range(halves):
            kept = factor * flags_ref[half * span_rows + t]
            state = kept * states[half] + x_ref[half, pl.ds(t, 1), :]
            mixed_ref[half, pl.ds(t, 1), :] = jnp.sum(residue * state, axis=0, keepdims=True)
            updated.append(state)
        return tuple(updated)

    ends = lax.fori_loop(0, span_rows, step, tuple(init_ref[half] for half in range(halves)), unroll=8)
    for half in range(halves):
        end_ref[half] = ends[half]


def run_scan(flags, values, factor, init, residue):
    halves, span_rows, channels = values.shape
    modes = factor.shape[0]
    vmem = pl.BlockSpec(memory_space=pltpu.VMEM)
    steps = halves * span_rows * modes * channels
    return pl.pallas_call(
        scan_kernel,
        out_shape=(
            jax.ShapeDtypeStruct((halves, span_rows, channels), jnp.float32),
            jax.ShapeDtypeStruct((halves, modes, channels), jnp.float32),
        ),
        in_specs=[pl.BlockSpec(memory_space=pltpu.SMEM), vmem, vmem, vmem, vmem],
        out_specs=(vmem, vmem),
        cost_estimate=pl.CostEstimate(
            flops=5 * steps, transcendentals=0, bytes_accessed=8 * halves * span_rows * channels
        ),
    )(flags, values, factor, init, residue)


def li_tables(doc_ids, li_decay, shard_rows):
    ctx_count, _, span_rows, span_starts, positions = span_layout(shard_rows)
    own_docs = jnp.stack([lax.dynamic_slice_in_dim(doc_ids, start, span_rows) for start in span_starts])
    padded = jnp.concatenate([doc_ids[:1], doc_ids])
    prior_docs = jnp.stack([lax.dynamic_slice_in_dim(padded, start, span_rows) for start in span_starts])
    flags = ((positions > 0) & (own_docs == prior_docs)).astype(jnp.float32).reshape(-1)
    block_count = 2 * ctx_count
    blocks = jnp.arange(block_count)
    end_docs = jnp.take(doc_ids, (blocks + 1) * span_rows - 1)
    targets = span_starts // span_rows
    entry_docs = jnp.take(doc_ids, jnp.clip(span_starts - 1, 0, None))
    linked = (blocks[None, :] < targets[:, None]) & (end_docs[None, :] == entry_docs[:, None])
    distance = jnp.where(linked, (targets[:, None] - blocks[None, :] - 1) * span_rows, 0).astype(jnp.float32)
    weights = jnp.exp(-li_decay[None, None] * distance[:, :, None, None]) * linked.astype(jnp.float32)[:, :, None, None]
    return flags, weights


def long_mix(product, li_decay, li_residue, tables):
    flags, weights = tables
    shard_rows, channels = product.shape
    span_rows = shard_rows // 2
    modes = li_decay.shape[0]
    factor = jnp.exp(-li_decay)
    values = product.reshape(2, span_rows, channels).astype(jnp.float32)
    zeros = jnp.zeros((2, modes, channels), jnp.float32)
    _, ends = run_scan(flags, values, factor, zeros, li_residue)
    gathered = lax.all_gather(ends, "ctx", axis=0, tiled=False)
    block_ends = jnp.concatenate([gathered[:, 0], gathered[::-1, 1]], 0)
    entry = jnp.sum(weights * block_ends[None], axis=1)
    mixed, _ = run_scan(flags, values, factor, entry, li_residue)
    return mixed.reshape(shard_rows, channels)


def body(
    tokens,
    mr_gain,
    mr_inproj,
    mr_outproj,
    mr_filter,
    li_gain,
    li_inproj,
    li_outproj,
    li_decay,
    li_residue,
    doc_ids,
):
    mr_piece, mr_columns = gather_layer_weights(mr_inproj, mr_outproj)
    li_piece = gather_weights(li_inproj)
    tables = li_tables(doc_ids, li_decay, tokens.shape[0])
    li_columns = outproj_columns(li_outproj)
    query, product = features_in(tokens, mr_gain, mr_piece)
    mixed = short_mix(product, mr_filter, doc_ids)
    stream = features_out(tokens, query, mixed, mr_columns)
    query, product = features_in(stream, li_gain, li_piece)
    return features_out(stream, query, long_mix(product, li_decay, li_residue, tables), li_columns)


def solution(mesh):
    ctx_count, ch_count = mesh.devices.shape
    pair_count = 2 if ch_count % 2 == 0 else 1
    view = jax.sharding.Mesh(
        mesh.devices.reshape(ctx_count, ch_count // pair_count, pair_count), ("ctx",) + CH
    )
    in_specs = (
        P("ctx", CH),
        P(),
        P("ctx", None, CH),
        P(CH, "ctx"),
        P(None, CH),
        P(),
        P("ctx", None, CH),
        P(CH, "ctx"),
        P(None, CH),
        P(None, CH),
        P(),
    )
    out_specs = P("ctx", CH)
    return jax.shard_map(body, mesh=view, in_specs=in_specs, out_specs=out_specs, check_vma=False)
```

```python
import math

import jax
import jax.numpy as jnp
from jax import lax
from jax.experimental import pallas as pl
from jax.experimental.pallas import tpu as pltpu
from jax.sharding import PartitionSpec as P


def extended(value, sides, width):
    for axis, dim in sides:
        count, length = (lax.axis_size(axis), value.shape[dim])
        up = [(i, (i + 1) % count) for i in range(count - 1)]
        down = [(j, i) for i, j in up]
        last = lax.slice_in_dim(value, length - width, length, axis=dim)
        initial = lax.slice_in_dim(value, 0, width, axis=dim)
        before = lax.ppermute(last, axis, up)
        after = lax.ppermute(initial, axis, down)
        value = jnp.concatenate([before, value, after], axis=dim)
    return value


CH = ("z", "yh")


def gather_channels(value):
    pair = lax.all_gather(value, "yh", axis=1, tiled=True)
    return lax.all_gather(pair, "z", axis=1, tiled=True)


def gather_weights(inproj):
    return lax.all_gather(inproj, "ctx", axis=0, tiled=True)


def features_in(stream, gain, piece):
    whole = gather_channels(stream)
    floats = whole.astype(jnp.float32)
    scaled = lax.rsqrt(jnp.mean(floats * floats, axis=1, keepdims=True) + 1e-06)
    normed = (floats * scaled * gain[None, :]).astype(jnp.bfloat16)
    channels = piece.shape[2]
    flat = piece.reshape(piece.shape[0], 3 * channels)
    joined = jnp.dot(normed, flat, preferred_element_type=jnp.float32).astype(jnp.bfloat16)
    product = (
        joined[:, channels : 2 * channels].astype(jnp.float32)
        * joined[:, 2 * channels :].astype(jnp.float32)
    ).astype(jnp.bfloat16)
    return (joined[:, :channels], product)


def swap_blocks(outproj):
    ctx_count, ch_count = (lax.axis_size("ctx"), lax.axis_size(CH))
    assert ctx_count == ch_count
    pairs = [(i * ch_count + c, c * ch_count + i) for i in range(ctx_count) for c in range(ch_count)]
    return lax.ppermute(outproj, ("ctx",) + CH, pairs)


def outproj_columns(outproj):
    return lax.all_gather(swap_blocks(outproj), "ctx", axis=0, tiled=True)


def gather_layer_weights(inproj, outproj):
    rows, parts, channels = inproj.shape
    joined = jnp.concatenate([inproj.reshape(rows, parts * channels), swap_blocks(outproj)], 1)
    whole = lax.all_gather(joined, "ctx", axis=0, tiled=True)
    piece = whole[:, : parts * channels].reshape(whole.shape[0], parts, channels)
    return piece, whole[:, parts * channels :]


def outproj_kernel(whole_ref, columns_ref, stream_ref, out_ref):
    width = columns_ref.shape[1]
    groups = whole_ref.shape[1] // width
    summed = None
    for group in range(groups):
        part = jnp.dot(
            whole_ref[:, group * width : (group + 1) * width],
            columns_ref[group * width : (group + 1) * width, :],
            preferred_element_type=jnp.float32,
        ).astype(jnp.bfloat16).astype(jnp.float32)
        summed = part if summed is None else summed + part
    out_ref[...] = (stream_ref[...].astype(jnp.float32) + summed).astype(jnp.bfloat16)


def project_groups(whole, columns, stream):
    rows, depth = whole.shape
    width = stream.shape[1]
    tile = 128 if rows % 128 == 0 else rows
    return pl.pallas_call(
        outproj_kernel,
        out_shape=jax.ShapeDtypeStruct(stream.shape, jnp.bfloat16),
        grid=(rows // tile,),
        in_specs=[
            pl.BlockSpec((tile, depth), lambda r: (r, 0)),
            pl.BlockSpec((depth, width), lambda r: (0, 0)),
            pl.BlockSpec((tile, width), lambda r: (r, 0)),
        ],
        out_specs=pl.BlockSpec((tile, width), lambda r: (r, 0)),
        cost_estimate=pl.CostEstimate(
            flops=2 * rows * depth * columns.shape[1],
            transcendentals=0,
            bytes_accessed=2 * (whole.size + columns.size + 2 * stream.size),
        ),
    )(whole, columns, stream)


def features_out(stream, query, mixed, columns):
    gated = (query.astype(jnp.float32) * mixed).astype(jnp.bfloat16)
    whole = gather_channels(gated)
    return project_groups(whole, columns, stream)


def span_layout(shard_rows):
    ctx_count = lax.axis_size("ctx")
    ctx_index = lax.axis_index("ctx")
    span_rows = shard_rows // 2
    span_starts = jnp.stack([ctx_index * span_rows, (2 * ctx_count - 1 - ctx_index) * span_rows])
    positions = span_starts[:, None] + jnp.arange(span_rows)[None, :]
    return (ctx_count, ctx_index, span_rows, span_starts, positions)


def short_mix(product, mr_filter, doc_ids):
    shard_rows, channels = product.shape
    ctx_count, ctx_index, span_rows, span_starts, _ = span_layout(shard_rows)
    tap_count = mr_filter.shape[0]
    reach_rows = tap_count - 1
    halves = product.reshape(2, span_rows, channels)
    tails = jnp.concatenate(
        [halves[1, span_rows - reach_rows :], halves[0, span_rows - reach_rows :]], 0
    )
    framed = extended(tails, (("ctx", 0),), reach_rows)
    before_upper = jnp.where(
        ctx_index == ctx_count - 1, halves[0, span_rows - reach_rows :], framed[3 * reach_rows :]
    )
    lower_window = jnp.concatenate([framed[:reach_rows], halves[0]], 0)
    upper_window = jnp.concatenate([before_upper, halves[1]], 0)
    windows = jnp.stack([lower_window, upper_window]).astype(jnp.float32)
    window_places = span_starts[:, None] - reach_rows + jnp.arange(reach_rows + span_rows)[None, :]
    window_docs = jnp.where(
        window_places >= 0, jnp.take(doc_ids, jnp.clip(window_places, 0, None)), -1
    )
    target_docs = window_docs[:, reach_rows:]
    tap_block = math.gcd(tap_count, 16)

    def tap_group(group_number, running):
        for offset in range(tap_block):
            tap_lag = group_number * tap_block + offset
            source = lax.dynamic_slice_in_dim(windows, reach_rows - tap_lag, span_rows, 1)
            source_docs = lax.dynamic_slice_in_dim(window_docs, reach_rows - tap_lag, span_rows, 1)
            weight = lax.dynamic_slice_in_dim(mr_filter, tap_lag, 1, 0)
            running = (
                running
                + jnp.where((source_docs == target_docs)[:, :, None], source, 0.0) * weight[None]
            )
        return running

    mixed = lax.fori_loop(
        0, tap_count // tap_block, tap_group, jnp.zeros((2, span_rows, channels), jnp.float32)
    )
    return mixed.reshape(shard_rows, channels)


def scan_kernel(flags_ref, x_ref, factor_ref, init_ref, residue_ref, mixed_ref, end_ref):
    halves, span_rows, _ = x_ref.shape
    factor = factor_ref[...]
    residue = residue_ref[...]

    def step(t, states):
        updated = []
        for half in range(halves):
            kept = factor * flags_ref[half * span_rows + t]
            state = kept * states[half] + x_ref[half, pl.ds(t, 1), :]
            mixed_ref[half, pl.ds(t, 1), :] = jnp.sum(residue * state, axis=0, keepdims=True)
            updated.append(state)
        return tuple(updated)

    ends = lax.fori_loop(0, span_rows, step, tuple(init_ref[half] for half in range(halves)), unroll=8)
    for half in range(halves):
        end_ref[half] = ends[half]


def run_scan(flags, values, factor, init, residue):
    halves, span_rows, channels = values.shape
    modes = factor.shape[0]
    vmem = pl.BlockSpec(memory_space=pltpu.VMEM)
    steps = halves * span_rows * modes * channels
    return pl.pallas_call(
        scan_kernel,
        out_shape=(
            jax.ShapeDtypeStruct((halves, span_rows, channels), jnp.float32),
            jax.ShapeDtypeStruct((halves, modes, channels), jnp.float32),
        ),
        in_specs=[pl.BlockSpec(memory_space=pltpu.SMEM), vmem, vmem, vmem, vmem],
        out_specs=(vmem, vmem),
        cost_estimate=pl.CostEstimate(
            flops=5 * steps, transcendentals=0, bytes_accessed=8 * halves * span_rows * channels
        ),
    )(flags, values, factor, init, residue)


def li_tables(doc_ids, li_decay, shard_rows):
    ctx_count, _, span_rows, span_starts, positions = span_layout(shard_rows)
    own_docs = jnp.stack([lax.dynamic_slice_in_dim(doc_ids, start, span_rows) for start in span_starts])
    padded = jnp.concatenate([doc_ids[:1], doc_ids])
    prior_docs = jnp.stack([lax.dynamic_slice_in_dim(padded, start, span_rows) for start in span_starts])
    flags = ((positions > 0) & (own_docs == prior_docs)).astype(jnp.float32).reshape(-1)
    block_count = 2 * ctx_count
    blocks = jnp.arange(block_count)
    end_docs = jnp.take(doc_ids, (blocks + 1) * span_rows - 1)
    targets = span_starts // span_rows
    entry_docs = jnp.take(doc_ids, jnp.clip(span_starts - 1, 0, None))
    linked = (blocks[None, :] < targets[:, None]) & (end_docs[None, :] == entry_docs[:, None])
    distance = jnp.where(linked, (targets[:, None] - blocks[None, :] - 1) * span_rows, 0).astype(jnp.float32)
    weights = jnp.exp(-li_decay[None, None] * distance[:, :, None, None]) * linked.astype(jnp.float32)[:, :, None, None]
    return flags, weights


def long_mix(product, li_decay, li_residue, tables):
    flags, weights = tables
    shard_rows, channels = product.shape
    span_rows = shard_rows // 2
    modes = li_decay.shape[0]
    factor = jnp.exp(-li_decay)
    values = product.reshape(2, span_rows, channels).astype(jnp.float32)
    zeros = jnp.zeros((2, modes, channels), jnp.float32)
    _, ends = run_scan(flags, values, factor, zeros, li_residue)
    gathered = lax.all_gather(ends, "ctx", axis=0, tiled=False)
    block_ends = jnp.concatenate([gathered[:, 0], gathered[::-1, 1]], 0)
    entry = jnp.sum(weights * block_ends[None], axis=1)
    mixed, _ = run_scan(flags, values, factor, entry, li_residue)
    return mixed.reshape(shard_rows, channels)


def body(
    tokens,
    mr_gain,
    mr_inproj,
    mr_outproj,
    mr_filter,
    li_gain,
    li_inproj,
    li_outproj,
    li_decay,
    li_residue,
    doc_ids,
):
    mr_piece, mr_columns = gather_layer_weights(mr_inproj, mr_outproj)
    li_piece = gather_weights(li_inproj)
    tables = li_tables(doc_ids, li_decay, tokens.shape[0])
    li_columns = outproj_columns(li_outproj)
    query, product = features_in(tokens, mr_gain, mr_piece)
    mixed = short_mix(product, mr_filter, doc_ids)
    stream = features_out(tokens, query, mixed, mr_columns)
    query, product = features_in(stream, li_gain, li_piece)
    return features_out(stream, query, long_mix(product, li_decay, li_residue, tables), li_columns)


def solution(mesh):
    ctx_count, ch_count = mesh.devices.shape
    pair_count = 2 if ch_count % 2 == 0 else 1
    view = jax.sharding.Mesh(
        mesh.devices.reshape(ctx_count, ch_count // pair_count, pair_count), ("ctx",) + CH
    )
    in_specs = (
        P("ctx", CH),
        P(),
        P("ctx", None, CH),
        P(CH, "ctx"),
        P(None, CH),
        P(),
        P("ctx", None, CH),
        P(CH, "ctx"),
        P(None, CH),
        P(None, CH),
        P(),
    )
    out_specs = P("ctx", CH)
    return jax.shard_map(body, mesh=view, in_specs=in_specs, out_specs=out_specs, check_vma=False)
```

```python
import math

import jax
import jax.numpy as jnp
from jax import lax
from jax.experimental import pallas as pl
from jax.experimental.pallas import tpu as pltpu
from jax.sharding import PartitionSpec as P


def extended(value, sides, width):
    for axis, dim in sides:
        count, length = (lax.axis_size(axis), value.shape[dim])
        up = [(i, (i + 1) % count) for i in range(count - 1)]
        down = [(j, i) for i, j in up]
        last = lax.slice_in_dim(value, length - width, length, axis=dim)
        initial = lax.slice_in_dim(value, 0, width, axis=dim)
        before = lax.ppermute(last, axis, up)
        after = lax.ppermute(initial, axis, down)
        value = jnp.concatenate([before, value, after], axis=dim)
    return value


CH = ("z", "yh")


def gather_channels(value):
    pair = lax.all_gather(value, "yh", axis=1, tiled=True)
    return lax.all_gather(pair, "z", axis=1, tiled=True)


def gather_weights(inproj):
    return lax.all_gather(inproj, "ctx", axis=0, tiled=True)


def features_in(stream, gain, piece):
    whole = gather_channels(stream)
    floats = whole.astype(jnp.float32)
    scaled = lax.rsqrt(jnp.mean(floats * floats, axis=1, keepdims=True) + 1e-06)
    normed = (floats * scaled * gain[None, :]).astype(jnp.bfloat16)
    channels = piece.shape[2]
    flat = piece.reshape(piece.shape[0], 3 * channels)
    joined = jnp.dot(normed, flat, preferred_element_type=jnp.float32).astype(jnp.bfloat16)
    product = (
        joined[:, channels : 2 * channels].astype(jnp.float32)
        * joined[:, 2 * channels :].astype(jnp.float32)
    ).astype(jnp.bfloat16)
    return (joined[:, :channels], product)


def swap_blocks(outproj):
    ctx_count, ch_count = (lax.axis_size("ctx"), lax.axis_size(CH))
    assert ctx_count == ch_count
    pairs = [(i * ch_count + c, c * ch_count + i) for i in range(ctx_count) for c in range(ch_count)]
    return lax.ppermute(outproj, ("ctx",) + CH, pairs)


def outproj_columns(outproj):
    return lax.all_gather(swap_blocks(outproj), "ctx", axis=0, tiled=True)


def gather_layer_weights(inproj, outproj):
    rows, parts, channels = inproj.shape
    joined = jnp.concatenate([inproj.reshape(rows, parts * channels), swap_blocks(outproj)], 1)
    whole = lax.all_gather(joined, "ctx", axis=0, tiled=True)
    piece = whole[:, : parts * channels].reshape(whole.shape[0], parts, channels)
    return piece, whole[:, parts * channels :]


def outproj_kernel(whole_ref, columns_ref, stream_ref, out_ref):
    width = columns_ref.shape[1]
    groups = whole_ref.shape[1] // width
    summed = None
    for group in range(groups):
        part = jnp.dot(
            whole_ref[:, group * width : (group + 1) * width],
            columns_ref[group * width : (group + 1) * width, :],
            preferred_element_type=jnp.float32,
        ).astype(jnp.bfloat16).astype(jnp.float32)
        summed = part if summed is None else summed + part
    out_ref[...] = (stream_ref[...].astype(jnp.float32) + summed).astype(jnp.bfloat16)


def project_groups(whole, columns, stream):
    vmem = pl.BlockSpec(memory_space=pltpu.VMEM)
    rows, depth = whole.shape
    return pl.pallas_call(
        outproj_kernel,
        out_shape=jax.ShapeDtypeStruct(stream.shape, jnp.bfloat16),
        in_specs=[vmem, vmem, vmem],
        out_specs=vmem,
        cost_estimate=pl.CostEstimate(
            flops=2 * rows * depth * columns.shape[1],
            transcendentals=0,
            bytes_accessed=2 * (whole.size + columns.size + 2 * stream.size),
        ),
    )(whole, columns, stream)


def features_out(stream, query, mixed, columns, gated=None):
    if gated is None:
        gated = (query.astype(jnp.float32) * mixed).astype(jnp.bfloat16)
    whole = gather_channels(gated)
    return project_groups(whole, columns, stream)


def span_layout(shard_rows):
    ctx_count = lax.axis_size("ctx")
    ctx_index = lax.axis_index("ctx")
    span_rows = shard_rows // 2
    span_starts = jnp.stack([ctx_index * span_rows, (2 * ctx_count - 1 - ctx_index) * span_rows])
    positions = span_starts[:, None] + jnp.arange(span_rows)[None, :]
    return (ctx_count, ctx_index, span_rows, span_starts, positions)


def short_mix(product, mr_filter, doc_ids):
    shard_rows, channels = product.shape
    ctx_count, ctx_index, span_rows, span_starts, _ = span_layout(shard_rows)
    tap_count = mr_filter.shape[0]
    reach_rows = tap_count - 1
    halves = product.reshape(2, span_rows, channels)
    tails = jnp.concatenate(
        [halves[1, span_rows - reach_rows :], halves[0, span_rows - reach_rows :]], 0
    )
    framed = extended(tails, (("ctx", 0),), reach_rows)
    before_upper = jnp.where(
        ctx_index == ctx_count - 1, halves[0, span_rows - reach_rows :], framed[3 * reach_rows :]
    )
    lower_window = jnp.concatenate([framed[:reach_rows], halves[0]], 0)
    upper_window = jnp.concatenate([before_upper, halves[1]], 0)
    windows = jnp.stack([lower_window, upper_window]).astype(jnp.float32)
    window_places = span_starts[:, None] - reach_rows + jnp.arange(reach_rows + span_rows)[None, :]
    window_docs = jnp.where(
        window_places >= 0, jnp.take(doc_ids, jnp.clip(window_places, 0, None)), -1
    )
    target_docs = window_docs[:, reach_rows:]
    tap_block = math.gcd(tap_count, 16)

    def tap_group(group_number, running):
        for offset in range(tap_block):
            tap_lag = group_number * tap_block + offset
            source = lax.dynamic_slice_in_dim(windows, reach_rows - tap_lag, span_rows, 1)
            source_docs = lax.dynamic_slice_in_dim(window_docs, reach_rows - tap_lag, span_rows, 1)
            weight = lax.dynamic_slice_in_dim(mr_filter, tap_lag, 1, 0)
            running = (
                running
                + jnp.where((source_docs == target_docs)[:, :, None], source, 0.0) * weight[None]
            )
        return running

    mixed = lax.fori_loop(
        0, tap_count // tap_block, tap_group, jnp.zeros((2, span_rows, channels), jnp.float32)
    )
    return mixed.reshape(shard_rows, channels)


def scan_kernel(flags_ref, x_ref, factor_ref, init_ref, residue_ref, *refs):
    if len(refs) == 4:
        query_ref, gated_ref, end_ref, rows_ref = refs
    else:
        query_ref = gated_ref = None
        end_ref, rows_ref = refs
    halves, span_rows, _ = x_ref.shape
    factor = factor_ref[...]
    residue = residue_ref[...]
    rows_ref[0] = x_ref[...].astype(jnp.float32)
    mixed_ref = rows_ref.at[1]

    def step(t, states):
        updated = []
        for half in range(halves):
            kept = factor * flags_ref[half * span_rows + t]
            state = kept * states[half] + rows_ref[0, half, pl.ds(t, 1), :]
            mixed_ref[half, pl.ds(t, 1), :] = jnp.sum(residue * state, axis=0, keepdims=True)
            updated.append(state)
        return tuple(updated)

    ends = lax.fori_loop(0, span_rows, step, tuple(init_ref[half] for half in range(halves)), unroll=8)
    for half in range(halves):
        end_ref[half] = ends[half]
    if gated_ref is not None:
        gated_ref[...] = (query_ref[...].astype(jnp.float32) * mixed_ref[...]).astype(jnp.bfloat16)


def run_scan(flags, values, factor, init, residue, query=None):
    halves, span_rows, channels = values.shape
    modes = factor.shape[0]
    vmem = pl.BlockSpec(memory_space=pltpu.VMEM)
    steps = halves * span_rows * modes * channels
    ends = jax.ShapeDtypeStruct((halves, modes, channels), jnp.float32)
    operands = [flags, values, factor, init, residue]
    out_shape = (ends,)
    if query is not None:
        operands.append(query)
        out_shape = (jax.ShapeDtypeStruct(query.shape, jnp.bfloat16), ends)
    return pl.pallas_call(
        scan_kernel,
        out_shape=out_shape,
        in_specs=[pl.BlockSpec(memory_space=pltpu.SMEM)] + [vmem] * (len(operands) - 1),
        out_specs=tuple(vmem for _ in out_shape),
        scratch_shapes=[pltpu.VMEM((2, halves, span_rows, channels), jnp.float32)],
        cost_estimate=pl.CostEstimate(
            flops=5 * steps, transcendentals=0, bytes_accessed=8 * halves * span_rows * channels
        ),
    )(*operands)


def li_tables(doc_ids, li_decay, shard_rows):
    ctx_count, _, span_rows, span_starts, positions = span_layout(shard_rows)
    own_docs = jnp.stack([lax.dynamic_slice_in_dim(doc_ids, start, span_rows) for start in span_starts])
    padded = jnp.concatenate([doc_ids[:1], doc_ids])
    prior_docs = jnp.stack([lax.dynamic_slice_in_dim(padded, start, span_rows) for start in span_starts])
    flags = ((positions > 0) & (own_docs == prior_docs)).astype(jnp.float32).reshape(-1)
    block_count = 2 * ctx_count
    blocks = jnp.arange(block_count)
    end_docs = jnp.take(doc_ids, (blocks + 1) * span_rows - 1)
    targets = span_starts // span_rows
    entry_docs = jnp.take(doc_ids, jnp.clip(span_starts - 1, 0, None))
    linked = (blocks[None, :] < targets[:, None]) & (end_docs[None, :] == entry_docs[:, None])
    distance = jnp.where(linked, (targets[:, None] - blocks[None, :] - 1) * span_rows, 0).astype(jnp.float32)
    weights = jnp.exp(-li_decay[None, None] * distance[:, :, None, None]) * linked.astype(jnp.float32)[:, :, None, None]
    return flags, weights


def long_mix(product, query, li_decay, li_residue, tables):
    flags, weights = tables
    shard_rows, channels = product.shape
    span_rows = shard_rows // 2
    modes = li_decay.shape[0]
    factor = jnp.exp(-li_decay)
    values = product.reshape(2, span_rows, channels)
    zeros = jnp.zeros((2, modes, channels), jnp.float32)
    (ends,) = run_scan(flags, values, factor, zeros, li_residue)
    gathered = lax.all_gather(ends, "ctx", axis=0, tiled=False)
    block_ends = jnp.concatenate([gathered[:, 0], gathered[::-1, 1]], 0)
    entry = jnp.sum(weights * block_ends[None], axis=1)
    gated, _ = run_scan(flags, values, factor, entry, li_residue, query.reshape(2, span_rows, channels))
    return gated.reshape(shard_rows, channels)


def body(
    tokens,
    mr_gain,
    mr_inproj,
    mr_outproj,
    mr_filter,
    li_gain,
    li_inproj,
    li_outproj,
    li_decay,
    li_residue,
    doc_ids,
):
    mr_piece, mr_columns = gather_layer_weights(mr_inproj, mr_outproj)
    li_piece = gather_weights(li_inproj)
    tables = li_tables(doc_ids, li_decay, tokens.shape[0])
    li_columns = outproj_columns(li_outproj)
    query, product = features_in(tokens, mr_gain, mr_piece)
    mixed = short_mix(product, mr_filter, doc_ids)
    stream = features_out(tokens, query, mixed, mr_columns)
    query, product = features_in(stream, li_gain, li_piece)
    return features_out(stream, None, None, li_columns, long_mix(product, query, li_decay, li_residue, tables))


def solution(mesh):
    ctx_count, ch_count = mesh.devices.shape
    pair_count = 2 if ch_count % 2 == 0 else 1
    view = jax.sharding.Mesh(
        mesh.devices.reshape(ctx_count, ch_count // pair_count, pair_count), ("ctx",) + CH
    )
    in_specs = (
        P("ctx", CH),
        P(),
        P("ctx", None, CH),
        P(CH, "ctx"),
        P(None, CH),
        P(),
        P("ctx", None, CH),
        P(CH, "ctx"),
        P(None, CH),
        P(None, CH),
        P(),
    )
    out_specs = P("ctx", CH)
    return jax.shard_map(body, mesh=view, in_specs=in_specs, out_specs=out_specs, check_vma=False)
```
